512 devices in a mesh: section: 8 (over x, y_hi), vocab: 64 (over z, y_lo, core).
Axes of the slice: x: 4, y: 4 (y_hi: 2, y_lo: 2; y = y_hi * 2 + y_lo), z: 16, core: 2. Of those that a mesh axis runs over, the one named last changes fastest.
Arguments:
- hidden: bfloat16 [512, 8192], P('vocab', 'section'), may hold values from -6 to 6
- head_weight: bfloat16 [98304, 8192], P('vocab', 'section'), may hold values from -3 to 3
- lengths: int32 [8], replicated, may hold values from 16 to 64
- pairing: int32 [4], replicated, may hold values from 0 to 3, each once
Outputs:
- hidden_grad: float32 [512, 8192], P('vocab', 'section')
- loss: float32 [], replicated
The draws below stay inside these ranges and needn't reach their ends.
Inputs may be any that keep to these rules, and one draw needn't show every extreme that they name: Every sequence has at least one live token; positions from lengths on are padding. `pairing`: a permutation: each document matches exactly one query.
All inputs are finite; a program needn't handle non-finite values.
Results may differ from the reference program's by a relative error of at most 0.0018.
Values may be sent and summed in bfloat16 or wider, within the bound.
No kernel may reach another device: no remote copies, remote signals or barrier semaphores. Data moves between devices by JAX's collectives and lax.ppermute only.
A program may use at most 64 MiB of HBM per device.

```python
import math
import jax
import jax.numpy as jnp
from jax import lax

D = 8192
NSEQ = 8
NQ = 4
TOKENS = 512
SEQ = 64
VOCAB = 98304


def draw_head_weight(key, part):
    key_rows = jax.random.fold_in(key, 11)
    key_vals = jax.random.fold_in(key, 12)
    scales = jnp.exp(jax.random.uniform(key_rows, (VOCAB, 1), jnp.float32, math.log(0.3), math.log(3.0)))
    values = jnp.clip(jax.random.normal(key_vals, (VOCAB, D), jnp.float32), -6.0, 6.0)
    return (values * scales * float(D) ** (-0.5)).astype(jnp.bfloat16)


def plant(result, key, least, top_value):
    dims = result.shape
    index_at = [jax.random.randint(jax.random.fold_in(key, axis), (), 0, dims[axis]) for axis in range(len(dims))]
    result = result.at[tuple(index_at)].set(least)
    longest = dims.index(max(dims))
    index_at[longest] = (index_at[longest] + 1) % dims[longest]
    return result.at[tuple(index_at)].set(top_value)


def levels(rng, extent, split, least, top_value):
    level = 1.0
    for dim, blocks in split:
        draws = jax.random.uniform(jax.random.fold_in(jax.random.fold_in(rng, 6), dim), (blocks,), jnp.float32, least / len(split), top_value / len(split))
        level = level * jnp.repeat(jnp.exp(draws), extent[dim] // blocks).reshape((-1,) + (1,) * (len(extent) - 1 - dim))
    return level


def noise(stream_key, extent, spread, reach, cuts=(), kind=jnp.bfloat16):
    factor_of = levels(stream_key, extent, cuts, -0.22, 0.18) if cuts else 1.0
    array = jax.random.normal(stream_key, extent, jnp.float32) * spread * factor_of
    return jnp.minimum(jnp.maximum(array, -reach), reach).astype(kind)


def setup_inputs(seed: int = 0) -> dict:
    streams_of = jax.random.split(jax.random.key(seed), 5)
    return {
        "hidden": noise(streams_of[0], (TOKENS, D), 1.0, 6.0, ((0, 64), (1, 8))),
        "head_weight": draw_head_weight(jax.random.fold_in(streams_of[4], 71), 0),
        "lengths": plant(jax.random.randint(streams_of[2], (NSEQ,), SEQ // 4, SEQ + 1), jax.random.fold_in(streams_of[2], 1), SEQ // 4, SEQ).astype(jnp.int32),
        "pairing": jax.random.permutation(streams_of[3], NQ).astype(jnp.int32),
    }


pool_temp = 0.5
score_temp = 0.02
grad_scale = 16.0
eps_norm = 1e-06

def reference(hidden, head_weight, lengths, pairing):
    logits = lax.dot_general(hidden, head_weight, (((1,), (1,)), ((), ())), preferred_element_type=jnp.float32)
    soft = jax.nn.softplus(logits)
    act = jnp.log1p(soft)
    positions = jnp.arange(SEQ, dtype=jnp.int32)
    live = (positions[None, :] < lengths[:, None]).astype(jnp.float32)
    expo = jnp.exp(act / pool_temp).reshape(NSEQ, SEQ, VOCAB) * live[:, :, None]
    totals = lax.optimization_barrier(jnp.sum(expo, axis=1))
    pooled = pool_temp * jnp.log(totals)
    queries = pooled[:NQ]
    documents = pooled[NQ:]
    dots = jnp.dot(queries, documents.T, precision=lax.Precision.HIGHEST)
    norms = lax.optimization_barrier(jnp.sum(pooled * pooled, axis=1))
    inv = lax.rsqrt(norms + eps_norm)
    inv_q = inv[:NQ]
    inv_d = inv[NQ:]
    scores = dots * inv_q[:, None] * inv_d[None, :] / score_temp
    weights = jnp.exp(scores)
    row_sum = lax.optimization_barrier(jnp.sum(weights, axis=1))
    probs = weights / row_sum[:, None]
    target = (jnp.arange(NQ, dtype=jnp.int32)[None, :] == pairing[:, None]).astype(jnp.float32)
    loss = jnp.sum(jnp.log(row_sum) - lax.optimization_barrier(jnp.sum(scores * target, axis=1)))
    dscore = grad_scale * (probs - target)
    gdots = dscore * inv_q[:, None] * inv_d[None, :] / score_temp
    dinv_q = lax.optimization_barrier(jnp.sum(dscore * dots * inv_d[None, :], axis=1)) / score_temp
    dinv_d = lax.optimization_barrier(jnp.sum(dscore * dots * inv_q[:, None], axis=0)) / score_temp
    dinv = jnp.concatenate([dinv_q, dinv_d])
    dnorm = -0.5 * dinv * inv * inv * inv
    dpool_q = jnp.dot(gdots, documents, precision=lax.Precision.HIGHEST) + 2.0 * dnorm[:NQ, None] * queries
    dpool_d = jnp.dot(gdots.T, queries, precision=lax.Precision.HIGHEST) + 2.0 * dnorm[NQ:, None] * documents
    dpooled = jnp.concatenate([dpool_q, dpool_d], axis=0)
    dact = (dpooled[:, None, :] * expo / totals[:, None, :]).reshape(NSEQ * SEQ, VOCAB)
    dlogit = (dact * jax.nn.sigmoid(logits) / (1.0 + soft)).astype(jnp.bfloat16)
    hidden_grad = jnp.dot(dlogit, head_weight, preferred_element_type=jnp.float32)
    return (hidden_grad, loss)
```

```python
import jax
import jax.numpy as jnp
from jax import lax
from jax.sharding import Mesh
from jax.sharding import PartitionSpec as P

NSEQ = 8


pool_temp = 0.5
score_temp = 0.02
grad_scale = 16.0
eps_norm = 1e-06

SEC = ("x", "yh")
VOC = ("z", "yl", "c")


def local(hidden, head_weight, lengths, pairing):
    half = NSEQ // 2
    gathered = lax.all_gather(hidden, ("yl", "c"), axis=0, tiled=True)
    gathered = lax.all_gather(gathered, "z", axis=0, tiled=True)
    partial_logits = lax.dot_general(
        gathered,
        head_weight,
        (((1,), (1,)), ((), ())),
        preferred_element_type=jnp.float32,
    )
    total_rows = partial_logits.shape[0]
    seq_len = total_rows // NSEQ
    logits = lax.psum_scatter(partial_logits, "x", scatter_dimension=1, tiled=True)
    logits = lax.psum_scatter(logits, "yh", scatter_dimension=1, tiled=True)
    columns = logits.shape[1]
    soft = jax.nn.softplus(logits)
    act = jnp.log1p(soft)
    positions = jnp.arange(seq_len, dtype=jnp.int32)
    live = (positions[None, :] < lengths[:, None]).astype(jnp.float32)
    expo = jnp.exp(act / pool_temp).reshape(NSEQ, seq_len, columns) * live[:, :, None]
    totals = jnp.sum(expo, axis=1)
    pooled = pool_temp * jnp.log(totals)
    queries = pooled[:half]
    documents = pooled[half:]
    dots_part = lax.dot_general(
        queries, documents, (((1,), (1,)), ((), ())), precision=lax.Precision.HIGHEST
    )
    norms_part = jnp.sum(pooled * pooled, axis=1)
    stats = (dots_part, norms_part)
    for axis in ("c", "yl", "yh", "x", "z"):
        stats = lax.psum(stats, axis)
    dots, norms = stats
    inv = lax.rsqrt(norms + eps_norm)
    inv_q = inv[:half]
    inv_d = inv[half:]
    scores = dots * inv_q[:, None] * inv_d[None, :] / score_temp
    weights = jnp.exp(scores)
    row_sum = jnp.sum(weights, axis=1)
    probs = weights / row_sum[:, None]
    target = (jnp.arange(half, dtype=jnp.int32)[None, :] == pairing[:, None]).astype(jnp.float32)
    loss = jnp.sum(jnp.log(row_sum) - jnp.sum(scores * target, axis=1))
    dscore = grad_scale * (probs - target)
    gdots = dscore * inv_q[:, None] * inv_d[None, :] / score_temp
    dinv_q = jnp.sum(dscore * dots * inv_d[None, :], axis=1) / score_temp
    dinv_d = jnp.sum(dscore * dots * inv_q[:, None], axis=0) / score_temp
    dinv = jnp.concatenate([dinv_q, dinv_d])
    dnorm = -0.5 * dinv * inv * inv * inv
    dpool_q = (
        jnp.dot(gdots, documents, precision=lax.Precision.HIGHEST)
        + 2.0 * dnorm[:half, None] * queries
    )
    dpool_d = (
        jnp.dot(gdots.T, queries, precision=lax.Precision.HIGHEST)
        + 2.0 * dnorm[half:, None] * documents
    )
    dpooled = jnp.concatenate([dpool_q, dpool_d], axis=0)
    dact = (dpooled[:, None, :] * expo / totals[:, None, :]).reshape(total_rows, columns)
    dlogit = (dact * jax.nn.sigmoid(logits) / (1.0 + soft)).astype(jnp.bfloat16)
    dlogit = lax.all_gather(dlogit, SEC, axis=1, tiled=True)
    partial_grad = jnp.dot(dlogit, head_weight, preferred_element_type=jnp.float32)
    hidden_grad = lax.psum_scatter(partial_grad, "z", scatter_dimension=0, tiled=True)
    hidden_grad = lax.psum_scatter(hidden_grad, ("yl", "c"), scatter_dimension=0, tiled=True)
    return (hidden_grad, loss)


def solution(mesh):
    n_sec, n_voc = mesh.devices.shape
    fine = Mesh(
        mesh.devices.reshape(n_sec // 2, 2, n_voc // 4, 2, 2), SEC + VOC
    )
    in_specs = (P(VOC, SEC), P(VOC, SEC), P(), P())
    out_specs = (P(VOC, SEC), P())
    return jax.shard_map(local, mesh=fine, in_specs=in_specs, out_specs=out_specs, check_vma=False)
```

```python
import jax
import jax.numpy as jnp
from jax import lax
from jax.sharding import Mesh
from jax.sharding import PartitionSpec as P

NSEQ = 8


pool_temp = 0.5
score_temp = 0.02
grad_scale = 16.0
eps_norm = 1e-06

SEC = ("x", "yh")
VOC = ("z", "yl", "c")


def _shift(v, axis, n, k):
    return lax.ppermute(v, axis, [(i, (i + k) % n) for i in range(n)])


def _ring_reduce_scatter(x, axis, n):
    me = lax.axis_index(axis)
    blocks = jnp.stack(jnp.split(x, n, axis=1))
    half = blocks.shape[-1] // 2
    fwd, bwd = blocks[..., :half], blocks[..., half:]

    def block(arr, k):
        return lax.dynamic_index_in_dim(arr, k % n, 0, keepdims=False)

    acc_f = block(fwd, me - 1)
    acc_b = block(bwd, me + 1)
    for step in range(1, n):
        acc_f = _shift(acc_f, axis, n, 1) + block(fwd, me - 1 - step)
        acc_b = _shift(acc_b, axis, n, -1) + block(bwd, me + 1 + step)
    return jnp.concatenate([acc_f, acc_b], axis=1)


def _pair_reduce_scatter(x, axis):
    lo, hi = jnp.split(x, 2, axis=1)
    first = lax.axis_index(axis) == 0
    keep = jnp.where(first, lo, hi)
    send = jnp.where(first, hi, lo)
    return keep + lax.ppermute(send, axis, [(0, 1), (1, 0)])


def _ring_gather_matmul(x, weight, axis, n):
    me = lax.axis_index(axis)
    rows = weight.shape[0] // n

    def term(v, owner):
        w = lax.dynamic_slice_in_dim(weight, (owner % n) * rows, rows, axis=0)
        return jnp.dot(v, w, preferred_element_type=jnp.float32)

    total = term(x, me)
    cur_f = cur_b = x
    n_f = n // 2
    n_b = n - 1 - n_f
    for step in range(max(n_f, n_b)):
        if step < n_f:
            cur_f = _shift(cur_f, axis, n, 1)
            total = total + term(cur_f, me - 1 - step)
        if step < n_b:
            cur_b = _shift(cur_b, axis, n, -1)
            total = total + term(cur_b, me + 1 + step)
    return total


def local(hidden, head_weight, lengths, pairing):
    half = NSEQ // 2
    gathered = lax.all_gather(hidden, ("yl", "c"), axis=0, tiled=True)
    gathered = lax.all_gather(gathered, "z", axis=0, tiled=True)
    partial_logits = lax.dot_general(
        gathered,
        head_weight,
        (((1,), (1,)), ((), ())),
        preferred_element_type=jnp.float32,
    )
    total_rows = partial_logits.shape[0]
    seq_len = total_rows // NSEQ
    n_x = lax.axis_size("x")
    logits = _ring_reduce_scatter(partial_logits, "x", n_x)
    logits = _pair_reduce_scatter(logits, "yh")
    columns = logits.shape[1]
    soft = jax.nn.softplus(logits)
    act = jnp.log1p(soft)
    positions = jnp.arange(seq_len, dtype=jnp.int32)
    live = (positions[None, :] < lengths[:, None]).astype(jnp.float32)
    expo = jnp.exp(act / pool_temp).reshape(NSEQ, seq_len, columns) * live[:, :, None]
    totals = jnp.sum(expo, axis=1)
    pooled = pool_temp * jnp.log(totals)
    queries = pooled[:half]
    documents = pooled[half:]
    dots_part = lax.dot_general(
        queries, documents, (((1,), (1,)), ((), ())), precision=lax.Precision.HIGHEST
    )
    norms_part = jnp.sum(pooled * pooled, axis=1)
    stats = (dots_part, norms_part)
    for axis in ("c", "yl", "yh", "x", "z"):
        stats = lax.psum(stats, axis)
    dots, norms = stats
    inv = lax.rsqrt(norms + eps_norm)
    inv_q = inv[:half]
    inv_d = inv[half:]
    scores = dots * inv_q[:, None] * inv_d[None, :] / score_temp
    weights = jnp.exp(scores)
    row_sum = jnp.sum(weights, axis=1)
    probs = weights / row_sum[:, None]
    target = (jnp.arange(half, dtype=jnp.int32)[None, :] == pairing[:, None]).astype(jnp.float32)
    loss = jnp.sum(jnp.log(row_sum) - jnp.sum(scores * target, axis=1))
    dscore = grad_scale * (probs - target)
    gdots = dscore * inv_q[:, None] * inv_d[None, :] / score_temp
    dinv_q = jnp.sum(dscore * dots * inv_d[None, :], axis=1) / score_temp
    dinv_d = jnp.sum(dscore * dots * inv_q[:, None], axis=0) / score_temp
    dinv = jnp.concatenate([dinv_q, dinv_d])
    dnorm = -0.5 * dinv * inv * inv * inv
    dpool_q = (
        jnp.dot(gdots, documents, precision=lax.Precision.HIGHEST)
        + 2.0 * dnorm[:half, None] * queries
    )
    dpool_d = (
        jnp.dot(gdots.T, queries, precision=lax.Precision.HIGHEST)
        + 2.0 * dnorm[half:, None] * documents
    )
    dpooled = jnp.concatenate([dpool_q, dpool_d], axis=0)
    dact = (dpooled[:, None, :] * expo / totals[:, None, :]).reshape(total_rows, columns)
    dlogit = (dact * jax.nn.sigmoid(logits) / (1.0 + soft)).astype(jnp.bfloat16)
    dlogit = lax.all_gather(dlogit, "yh", axis=1, tiled=True)
    partial_grad = _ring_gather_matmul(dlogit, head_weight, "x", n_x)
    hidden_grad = lax.psum_scatter(partial_grad, "z", scatter_dimension=0, tiled=True)
    hidden_grad = lax.psum_scatter(hidden_grad, ("yl", "c"), scatter_dimension=0, tiled=True)
    return (hidden_grad, loss)


def solution(mesh):
    n_sec, n_voc = mesh.devices.shape
    fine = Mesh(
        mesh.devices.reshape(n_sec // 2, 2, n_voc // 4, 2, 2), SEC + VOC
    )
    in_specs = (P(VOC, SEC), P(VOC, SEC), P(), P())
    out_specs = (P(VOC, SEC), P())
    return jax.shard_map(local, mesh=fine, in_specs=in_specs, out_specs=out_specs, check_vma=False)
```

```python
import jax
import jax.numpy as jnp
from jax import lax
from jax.sharding import Mesh
from jax.sharding import PartitionSpec as P

NSEQ = 8


pool_temp = 0.5
score_temp = 0.02
grad_scale = 16.0
eps_norm = 1e-06

SEC = ("x", "yh")
VOC = ("z", "yl", "c")


def _shift(v, axis, n, k):
    return lax.ppermute(v, axis, [(i, (i + k) % n) for i in range(n)])


def _ring_matmul_reduce_scatter(lhs, weight, axis, n):
    me = lax.axis_index(axis)
    rows = weight.shape[0] // n
    half = rows // 2

    def term(k, offset):
        w = lax.dynamic_slice_in_dim(weight, (k % n) * rows + offset, half, axis=0)
        return lax.dot_general(
            lhs, w, (((1,), (1,)), ((), ())), preferred_element_type=jnp.float32
        )

    acc_f = term(me - 1, 0)
    acc_b = term(me + 1, half)
    for step in range(1, n):
        acc_f = _shift(acc_f, axis, n, 1) + term(me - 1 - step, 0)
        acc_b = _shift(acc_b, axis, n, -1) + term(me + 1 + step, half)
    return jnp.concatenate([acc_f, acc_b], axis=1)


def _pair_reduce_scatter(x, axis, dim):
    lo, hi = jnp.split(x, 2, axis=dim)
    first = lax.axis_index(axis) == 0
    keep = jnp.where(first, lo, hi)
    send = jnp.where(first, hi, lo)
    return keep + lax.ppermute(send, axis, [(0, 1), (1, 0)])


def _ring_gather_matmul(x, weight, axis, n):
    me = lax.axis_index(axis)
    rows = weight.shape[0] // n

    def term(v, owner):
        w = lax.dynamic_slice_in_dim(weight, (owner % n) * rows, rows, axis=0)
        return jnp.dot(v, w, preferred_element_type=jnp.float32)

    total = term(x, me)
    cur_f = cur_b = x
    n_f = n // 2
    n_b = n - 1 - n_f
    for step in range(max(n_f, n_b)):
        if step < n_f:
            cur_f = _shift(cur_f, axis, n, 1)
            total = total + term(cur_f, me - 1 - step)
        if step < n_b:
            cur_b = _shift(cur_b, axis, n, -1)
            total = total + term(cur_b, me + 1 + step)
    return total


def local(hidden, head_weight, lengths, pairing):
    half = NSEQ // 2
    gathered = lax.all_gather(hidden, ("yl", "c"), axis=0, tiled=True)
    gathered = lax.all_gather(gathered, "z", axis=0, tiled=True)
    total_rows = gathered.shape[0]
    seq_len = total_rows // NSEQ
    n_x = lax.axis_size("x")
    logits = _ring_matmul_reduce_scatter(gathered, head_weight, "x", n_x)
    logits = _pair_reduce_scatter(logits, "yh", 1)
    columns = logits.shape[1]
    soft = jax.nn.softplus(logits)
    act = jnp.log1p(soft)
    positions = jnp.arange(seq_len, dtype=jnp.int32)
    live = (positions[None, :] < lengths[:, None]).astype(jnp.float32)
    expo = jnp.exp(act / pool_temp).reshape(NSEQ, seq_len, columns) * live[:, :, None]
    totals = jnp.sum(expo, axis=1)
    pooled = pool_temp * jnp.log(totals)
    queries = pooled[:half]
    documents = pooled[half:]
    dots_part = lax.dot_general(
        queries, documents, (((1,), (1,)), ((), ())), precision=lax.Precision.HIGHEST
    )
    norms_part = jnp.sum(pooled * pooled, axis=1)
    stats = (dots_part, norms_part)
    for axis in ("c", "yl", "yh", "x", "z"):
        stats = lax.psum(stats, axis)
    dots, norms = stats
    inv = lax.rsqrt(norms + eps_norm)
    inv_q = inv[:half]
    inv_d = inv[half:]
    scores = dots * inv_q[:, None] * inv_d[None, :] / score_temp
    weights = jnp.exp(scores)
    row_sum = jnp.sum(weights, axis=1)
    probs = weights / row_sum[:, None]
    target = (jnp.arange(half, dtype=jnp.int32)[None, :] == pairing[:, None]).astype(jnp.float32)
    loss = jnp.sum(jnp.log(row_sum) - jnp.sum(scores * target, axis=1))
    dscore = grad_scale * (probs - target)
    gdots = dscore * inv_q[:, None] * inv_d[None, :] / score_temp
    dinv_q = jnp.sum(dscore * dots * inv_d[None, :], axis=1) / score_temp
    dinv_d = jnp.sum(dscore * dots * inv_q[:, None], axis=0) / score_temp
    dinv = jnp.concatenate([dinv_q, dinv_d])
    dnorm = -0.5 * dinv * inv * inv * inv
    dpool_q = (
        jnp.dot(gdots, documents, precision=lax.Precision.HIGHEST)
        + 2.0 * dnorm[:half, None] * queries
    )
    dpool_d = (
        jnp.dot(gdots.T, queries, precision=lax.Precision.HIGHEST)
        + 2.0 * dnorm[half:, None] * documents
    )
    dpooled = jnp.concatenate([dpool_q, dpool_d], axis=0)
    dact = (dpooled[:, None, :] * expo / totals[:, None, :]).reshape(total_rows, columns)
    dlogit = (dact * jax.nn.sigmoid(logits) / (1.0 + soft)).astype(jnp.bfloat16)
    dlogit = lax.all_gather(dlogit, "yh", axis=1, tiled=True)
    partial_grad = _ring_gather_matmul(dlogit, head_weight, "x", n_x)
    hidden_grad = lax.psum_scatter(partial_grad, "z", scatter_dimension=0, tiled=True)
    hidden_grad = _pair_reduce_scatter(hidden_grad, "yl", 0)
    hidden_grad = _pair_reduce_scatter(hidden_grad, "c", 0)
    return (hidden_grad, loss)


def solution(mesh):
    n_sec, n_voc = mesh.devices.shape
    fine = Mesh(
        mesh.devices.reshape(n_sec // 2, 2, n_voc // 4, 2, 2), SEC + VOC
    )
    in_specs = (P(VOC, SEC), P(VOC, SEC), P(), P())
    out_specs = (P(VOC, SEC), P())
    return jax.shard_map(local, mesh=fine, in_specs=in_specs, out_specs=out_specs, check_vma=False)
```

```python
import jax
import jax.numpy as jnp
from jax import lax
from jax.sharding import Mesh
from jax.sharding import PartitionSpec as P

NSEQ = 8


pool_temp = 0.5
score_temp = 0.02
grad_scale = 16.0
eps_norm = 1e-06

SEC = ("x", "yh")
VOC = ("z", "yl", "c")


def _members(axes):
    axes = axes if isinstance(axes, tuple) else (axes,)
    n = 1
    for a in axes:
        n *= lax.axis_size(a)
    return n


def _all_gather_a2a(x, axes):
    n = _members(axes)
    copies = jnp.broadcast_to(x[None], (n,) + x.shape)
    out = lax.all_to_all(copies, axes, 0, 0, tiled=True)
    return out.reshape((n * x.shape[0],) + x.shape[1:])


def _reduce_scatter_a2a(x, axes):
    n = _members(axes)
    rows, cols = x.shape
    blocks = x.reshape(rows, n, cols // n).transpose(1, 0, 2)
    return jnp.sum(lax.all_to_all(blocks, axes, 0, 0, tiled=True), axis=0)


def _all_reduce_a2a(x, axes):
    n = _members(axes)
    copies = jnp.broadcast_to(x[None], (n,) + x.shape)
    return jnp.sum(lax.all_to_all(copies, axes, 0, 0, tiled=True), axis=0)


def _shift(v, axis, n, k):
    return lax.ppermute(v, axis, [(i, (i + k) % n) for i in range(n)])


def _pair_reduce_scatter(x, axis, dim):
    lo, hi = jnp.split(x, 2, axis=dim)
    first = lax.axis_index(axis) == 0
    keep = jnp.where(first, lo, hi)
    send = jnp.where(first, hi, lo)
    return keep + lax.ppermute(send, axis, [(0, 1), (1, 0)])


def _ring_gather_matmul(x, weight, axis, n):
    me = lax.axis_index(axis)
    rows = weight.shape[0] // n

    def term(v, owner):
        w = lax.dynamic_slice_in_dim(weight, (owner % n) * rows, rows, axis=0)
        return jnp.dot(v, w, preferred_element_type=jnp.float32)

    total = term(x, me)
    cur_f = cur_b = x
    n_f = n // 2
    n_b = n - 1 - n_f
    for step in range(max(n_f, n_b)):
        if step < n_f:
            cur_f = _shift(cur_f, axis, n, 1)
            total = total + term(cur_f, me - 1 - step)
        if step < n_b:
            cur_b = _shift(cur_b, axis, n, -1)
            total = total + term(cur_b, me + 1 + step)
    return total


def local(hidden, head_weight, lengths, pairing):
    half = NSEQ // 2
    gathered = lax.all_gather(hidden, ("yl", "c"), axis=0, tiled=True)
    gathered = _all_gather_a2a(gathered, "z")
    total_rows = gathered.shape[0]
    seq_len = total_rows // NSEQ
    n_x = lax.axis_size("x")
    partial_logits = lax.dot_general(
        gathered,
        head_weight,
        (((1,), (1,)), ((), ())),
        preferred_element_type=jnp.float32,
    )
    logits = _reduce_scatter_a2a(partial_logits, SEC)
    columns = logits.shape[1]
    soft = jax.nn.softplus(logits)
    act = jnp.log1p(soft)
    positions = jnp.arange(seq_len, dtype=jnp.int32)
    live = (positions[None, :] < lengths[:, None]).astype(jnp.float32)
    expo = jnp.exp(act / pool_temp).reshape(NSEQ, seq_len, columns) * live[:, :, None]
    totals = jnp.sum(expo, axis=1)
    pooled = pool_temp * jnp.log(totals)
    queries = pooled[:half]
    documents = pooled[half:]
    dots_part = lax.dot_general(
        queries, documents, (((1,), (1,)), ((), ())), precision=lax.Precision.HIGHEST
    )
    norms_part = jnp.sum(pooled * pooled, axis=1)
    stats = jnp.concatenate([dots_part.reshape(-1), norms_part])
    for axes in (("yl", "c"), SEC, "z"):
        stats = _all_reduce_a2a(stats, axes)
    dots = stats[: half * half].reshape(half, half)
    norms = stats[half * half :]
    inv = lax.rsqrt(norms + eps_norm)
    inv_q = inv[:half]
    inv_d = inv[half:]
    scores = dots * inv_q[:, None] * inv_d[None, :] / score_temp
    weights = jnp.exp(scores)
    row_sum = jnp.sum(weights, axis=1)
    probs = weights / row_sum[:, None]
    target = (jnp.arange(half, dtype=jnp.int32)[None, :] == pairing[:, None]).astype(jnp.float32)
    loss = jnp.sum(jnp.log(row_sum) - jnp.sum(scores * target, axis=1))
    dscore = grad_scale * (probs - target)
    gdots = dscore * inv_q[:, None] * inv_d[None, :] / score_temp
    dinv_q = jnp.sum(dscore * dots * inv_d[None, :], axis=1) / score_temp
    dinv_d = jnp.sum(dscore * dots * inv_q[:, None], axis=0) / score_temp
    dinv = jnp.concatenate([dinv_q, dinv_d])
    dnorm = -0.5 * dinv * inv * inv * inv
    dpool_q = (
        jnp.dot(gdots, documents, precision=lax.Precision.HIGHEST)
        + 2.0 * dnorm[:half, None] * queries
    )
    dpool_d = (
        jnp.dot(gdots.T, queries, precision=lax.Precision.HIGHEST)
        + 2.0 * dnorm[half:, None] * documents
    )
    dpooled = jnp.concatenate([dpool_q, dpool_d], axis=0)
    dact = (dpooled[:, None, :] * expo / totals[:, None, :]).reshape(total_rows, columns)
    dlogit = (dact * jax.nn.sigmoid(logits) / (1.0 + soft)).astype(jnp.bfloat16)
    dlogit = lax.all_gather(dlogit, "yh", axis=1, tiled=True)
    partial_grad = _ring_gather_matmul(dlogit, head_weight, "x", n_x)
    hidden_grad = lax.psum_scatter(partial_grad, "z", scatter_dimension=0, tiled=True)
    hidden_grad = _pair_reduce_scatter(hidden_grad, "yl", 0)
    hidden_grad = _pair_reduce_scatter(hidden_grad, "c", 0)
    return (hidden_grad, loss)


def solution(mesh):
    n_sec, n_voc = mesh.devices.shape
    fine = Mesh(
        mesh.devices.reshape(n_sec // 2, 2, n_voc // 4, 2, 2), SEC + VOC
    )
    in_specs = (P(VOC, SEC), P(VOC, SEC), P(), P())
    out_specs = (P(VOC, SEC), P())
    return jax.shard_map(local, mesh=fine, in_specs=in_specs, out_specs=out_specs, check_vma=False)
```

```python
import jax
import jax.numpy as jnp
from jax import lax
from jax.sharding import Mesh
from jax.sharding import PartitionSpec as P

NSEQ = 8


pool_temp = 0.5
score_temp = 0.02
grad_scale = 16.0
eps_norm = 1e-06

SEC = ("x", "yh")
Z = ("zh", "zl")
VOC = Z + ("yl", "c")


def _members(axes):
    axes = axes if isinstance(axes, tuple) else (axes,)
    n = 1
    for a in axes:
        n *= lax.axis_size(a)
    return n


def _all_gather_a2a(x, axes):
    n = _members(axes)
    copies = jnp.broadcast_to(x[None], (n,) + x.shape)
    out = lax.all_to_all(copies, axes, 0, 0, tiled=True)
    return out.reshape((n * x.shape[0],) + x.shape[1:])


def _reduce_scatter_a2a(x, axes):
    n = _members(axes)
    rows, cols = x.shape
    blocks = x.reshape(rows, n, cols // n).transpose(1, 0, 2)
    return jnp.sum(lax.all_to_all(blocks, axes, 0, 0, tiled=True), axis=0)


def _all_reduce_a2a(x, axes):
    n = _members(axes)
    copies = jnp.broadcast_to(x[None], (n,) + x.shape)
    return jnp.sum(lax.all_to_all(copies, axes, 0, 0, tiled=True), axis=0)


def _shift(v, axis, n, k):
    return lax.ppermute(v, axis, [(i, (i + k) % n) for i in range(n)])


def _pair_reduce_scatter(x, axis, dim):
    lo, hi = jnp.split(x, 2, axis=dim)
    first = lax.axis_index(axis) == 0
    keep = jnp.where(first, lo, hi)
    send = jnp.where(first, hi, lo)
    return keep + lax.ppermute(send, axis, [(0, 1), (1, 0)])


def _ring_gather_matmul(x, weight, axis, n):
    me = lax.axis_index(axis)
    rows = weight.shape[0] // n

    def term(v, owner):
        w = lax.dynamic_slice_in_dim(weight, (owner % n) * rows, rows, axis=0)
        return jnp.dot(v, w, preferred_element_type=jnp.float32)

    total = term(x, me)
    cur_f = cur_b = x
    n_f = n // 2
    n_b = n - 1 - n_f
    for step in range(max(n_f, n_b)):
        if step < n_f:
            cur_f = _shift(cur_f, axis, n, 1)
            total = total + term(cur_f, me - 1 - step)
        if step < n_b:
            cur_b = _shift(cur_b, axis, n, -1)
            total = total + term(cur_b, me + 1 + step)
    return total


def local(hidden, head_weight, lengths, pairing):
    half = NSEQ // 2
    gathered = lax.all_gather(hidden, ("yl", "c"), axis=0, tiled=True)
    gathered = _all_gather_a2a(gathered, "zh")
    n_zh = lax.axis_size("zh")
    gathered = _all_gather_a2a(gathered, "zl")
    gathered = gathered.reshape(-1, n_zh, gathered.shape[0] // (n_zh * lax.axis_size("zl")), gathered.shape[1])
    gathered = gathered.transpose(1, 0, 2, 3).reshape(-1, gathered.shape[-1])
    total_rows = gathered.shape[0]
    seq_len = total_rows // NSEQ
    n_x = lax.axis_size("x")
    partial_logits = lax.dot_general(
        gathered,
        head_weight,
        (((1,), (1,)), ((), ())),
        preferred_element_type=jnp.float32,
    )
    logits = _reduce_scatter_a2a(partial_logits, SEC)
    columns = logits.shape[1]
    soft = jax.nn.softplus(logits)
    act = jnp.log1p(soft)
    positions = jnp.arange(seq_len, dtype=jnp.int32)
    live = (positions[None, :] < lengths[:, None]).astype(jnp.float32)
    expo = jnp.exp(act / pool_temp).reshape(NSEQ, seq_len, columns) * live[:, :, None]
    totals = jnp.sum(expo, axis=1)
    pooled = pool_temp * jnp.log(totals)
    queries = pooled[:half]
    documents = pooled[half:]
    dots_part = lax.dot_general(
        queries, documents, (((1,), (1,)), ((), ())), precision=lax.Precision.HIGHEST
    )
    norms_part = jnp.sum(pooled * pooled, axis=1)
    stats = jnp.concatenate([dots_part.reshape(-1), norms_part])
    for axes in (("yl", "c"), SEC, Z):
        stats = _all_reduce_a2a(stats, axes)
    dots = stats[: half * half].reshape(half, half)
    norms = stats[half * half :]
    inv = lax.rsqrt(norms + eps_norm)
    inv_q = inv[:half]
    inv_d = inv[half:]
    scores = dots * inv_q[:, None] * inv_d[None, :] / score_temp
    weights = jnp.exp(scores)
    row_sum = jnp.sum(weights, axis=1)
    probs = weights / row_sum[:, None]
    target = (jnp.arange(half, dtype=jnp.int32)[None, :] == pairing[:, None]).astype(jnp.float32)
    loss = jnp.sum(jnp.log(row_sum) - jnp.sum(scores * target, axis=1))
    dscore = grad_scale * (probs - target)
    gdots = dscore * inv_q[:, None] * inv_d[None, :] / score_temp
    dinv_q = jnp.sum(dscore * dots * inv_d[None, :], axis=1) / score_temp
    dinv_d = jnp.sum(dscore * dots * inv_q[:, None], axis=0) / score_temp
    dinv = jnp.concatenate([dinv_q, dinv_d])
    dnorm = -0.5 * dinv * inv * inv * inv
    dpool_q = (
        jnp.dot(gdots, documents, precision=lax.Precision.HIGHEST)
        + 2.0 * dnorm[:half, None] * queries
    )
    dpool_d = (
        jnp.dot(gdots.T, queries, precision=lax.Precision.HIGHEST)
        + 2.0 * dnorm[half:, None] * documents
    )
    dpooled = jnp.concatenate([dpool_q, dpool_d], axis=0)
    dact = (dpooled[:, None, :] * expo / totals[:, None, :]).reshape(total_rows, columns)
    dlogit = (dact * jax.nn.sigmoid(logits) / (1.0 + soft)).astype(jnp.bfloat16)
    dlogit = lax.all_gather(dlogit, "yh", axis=1, tiled=True)
    partial_grad = _ring_gather_matmul(dlogit, head_weight, "x", n_x)
    hidden_grad = lax.psum_scatter(partial_grad, Z, scatter_dimension=0, tiled=True)
    hidden_grad = _pair_reduce_scatter(hidden_grad, "yl", 0)
    hidden_grad = _pair_reduce_scatter(hidden_grad, "c", 0)
    return (hidden_grad, loss)


def solution(mesh):
    n_sec, n_voc = mesh.devices.shape
    fine = Mesh(
        mesh.devices.reshape(n_sec // 2, 2, n_voc // 16, 4, 2, 2), SEC + VOC
    )
    in_specs = (P(VOC, SEC), P(VOC, SEC), P(), P())
    out_specs = (P(VOC, SEC), P())
    return jax.shard_map(local, mesh=fine, in_specs=in_specs, out_specs=out_specs, check_vma=False)
```

```python
import jax
import jax.numpy as jnp
from jax import lax
from jax.sharding import Mesh
from jax.sharding import PartitionSpec as P

NSEQ = 8


pool_temp = 0.5
score_temp = 0.02
grad_scale = 16.0
eps_norm = 1e-06

SEC = ("x", "yh")
Z = ("zh", "zl")
VOC = Z + ("yl", "c")


def _members(axes):
    axes = axes if isinstance(axes, tuple) else (axes,)
    n = 1
    for a in axes:
        n *= lax.axis_size(a)
    return n


def _all_gather_a2a(x, axes):
    n = _members(axes)
    copies = jnp.broadcast_to(x[None], (n,) + x.shape)
    out = lax.all_to_all(copies, axes, 0, 0, tiled=True)
    return out.reshape((n * x.shape[0],) + x.shape[1:])


def _reduce_scatter_a2a(x, axes):
    n = _members(axes)
    rows, cols = x.shape
    blocks = x.reshape(rows, n, cols // n).transpose(1, 0, 2)
    return jnp.sum(lax.all_to_all(blocks, axes, 0, 0, tiled=True), axis=0)


def _all_reduce_a2a(x, axes):
    n = _members(axes)
    copies = jnp.broadcast_to(x[None], (n,) + x.shape)
    return jnp.sum(lax.all_to_all(copies, axes, 0, 0, tiled=True), axis=0)


def _shift(v, axis, n, k):
    return lax.ppermute(v, axis, [(i, (i + k) % n) for i in range(n)])


def _pair_reduce_scatter(x, axis, dim):
    lo, hi = jnp.split(x, 2, axis=dim)
    first = lax.axis_index(axis) == 0
    keep = jnp.where(first, lo, hi)
    send = jnp.where(first, hi, lo)
    return keep + lax.ppermute(send, axis, [(0, 1), (1, 0)])


def _ring_gather_matmul(x, weight, axis, n):
    me = lax.axis_index(axis)
    rows = weight.shape[0] // n

    def term(v, owner):
        w = lax.dynamic_slice_in_dim(weight, (owner % n) * rows, rows, axis=0)
        return jnp.dot(v, w, preferred_element_type=jnp.float32)

    total = term(x, me)
    cur_f = cur_b = x
    n_f = n // 2
    n_b = n - 1 - n_f
    for step in range(max(n_f, n_b)):
        if step < n_f:
            cur_f = _shift(cur_f, axis, n, 1)
            total = total + term(cur_f, me - 1 - step)
        if step < n_b:
            cur_b = _shift(cur_b, axis, n, -1)
            total = total + term(cur_b, me + 1 + step)
    return total


def local(hidden, head_weight, lengths, pairing):
    half = NSEQ // 2
    near = ("zl", "yl", "c")
    gathered = _all_gather_a2a(hidden, "zh")
    n_zh = lax.axis_size("zh")
    gathered = _all_gather_a2a(gathered, near)
    gathered = gathered.reshape(_members(near), n_zh, hidden.shape[0], hidden.shape[1])
    gathered = gathered.transpose(1, 0, 2, 3).reshape(-1, hidden.shape[1])
    total_rows = gathered.shape[0]
    seq_len = total_rows // NSEQ
    n_x = lax.axis_size("x")
    partial_logits = lax.dot_general(
        gathered,
        head_weight,
        (((1,), (1,)), ((), ())),
        preferred_element_type=jnp.float32,
    )
    logits = _reduce_scatter_a2a(partial_logits, SEC)
    columns = logits.shape[1]
    soft = jax.nn.softplus(logits)
    act = jnp.log1p(soft)
    positions = jnp.arange(seq_len, dtype=jnp.int32)
    live = (positions[None, :] < lengths[:, None]).astype(jnp.float32)
    expo = jnp.exp(act / pool_temp).reshape(NSEQ, seq_len, columns) * live[:, :, None]
    totals = jnp.sum(expo, axis=1)
    pooled = pool_temp * jnp.log(totals)
    queries = pooled[:half]
    documents = pooled[half:]
    dots_part = lax.dot_general(
        queries, documents, (((1,), (1,)), ((), ())), precision=lax.Precision.HIGHEST
    )
    norms_part = jnp.sum(pooled * pooled, axis=1)
    stats = jnp.concatenate([dots_part.reshape(-1), norms_part])
    for axes in (VOC, SEC):
        stats = _all_reduce_a2a(stats, axes)
    dots = stats[: half * half].reshape(half, half)
    norms = stats[half * half :]
    inv = lax.rsqrt(norms + eps_norm)
    inv_q = inv[:half]
    inv_d = inv[half:]
    scores = dots * inv_q[:, None] * inv_d[None, :] / score_temp
    weights = jnp.exp(scores)
    row_sum = jnp.sum(weights, axis=1)
    probs = weights / row_sum[:, None]
    target = (jnp.arange(half, dtype=jnp.int32)[None, :] == pairing[:, None]).astype(jnp.float32)
    loss = jnp.sum(jnp.log(row_sum) - jnp.sum(scores * target, axis=1))
    dscore = grad_scale * (probs - target)
    gdots = dscore * inv_q[:, None] * inv_d[None, :] / score_temp
    dinv_q = jnp.sum(dscore * dots * inv_d[None, :], axis=1) / score_temp
    dinv_d = jnp.sum(dscore * dots * inv_q[:, None], axis=0) / score_temp
    dinv = jnp.concatenate([dinv_q, dinv_d])
    dnorm = -0.5 * dinv * inv * inv * inv
    dpool_q = (
        jnp.dot(gdots, documents, precision=lax.Precision.HIGHEST)
        + 2.0 * dnorm[:half, None] * queries
    )
    dpool_d = (
        jnp.dot(gdots.T, queries, precision=lax.Precision.HIGHEST)
        + 2.0 * dnorm[half:, None] * documents
    )
    dpooled = jnp.concatenate([dpool_q, dpool_d], axis=0)
    dact = (dpooled[:, None, :] * expo / totals[:, None, :]).reshape(total_rows, columns)
    dlogit = (dact * jax.nn.sigmoid(logits) / (1.0 + soft)).astype(jnp.bfloat16)
    dlogit = lax.all_gather(dlogit, "yh", axis=1, tiled=True)
    partial_grad = _ring_gather_matmul(dlogit, head_weight, "x", n_x)
    hidden_grad = lax.psum_scatter(partial_grad, Z, scatter_dimension=0, tiled=True)
    hidden_grad = _pair_reduce_scatter(hidden_grad, "yl", 0)
    hidden_grad = _pair_reduce_scatter(hidden_grad, "c", 0)
    return (hidden_grad, loss)


def solution(mesh):
    n_sec, n_voc = mesh.devices.shape
    fine = Mesh(
        mesh.devices.reshape(n_sec // 2, 2, n_voc // 16, 4, 2, 2), SEC + VOC
    )
    in_specs = (P(VOC, SEC), P(VOC, SEC), P(), P())
    out_specs = (P(VOC, SEC), P())
    return jax.shard_map(local, mesh=fine, in_specs=in_specs, out_specs=out_specs, check_vma=False)
```

```python
import jax
import jax.numpy as jnp
from jax import lax
from jax.sharding import Mesh
from jax.sharding import PartitionSpec as P

NSEQ = 8


pool_temp = 0.5
score_temp = 0.02
grad_scale = 16.0
eps_norm = 1e-06

SEC = ("x", "yh")
Z = ("zh", "zl")
VOC = Z + ("yl", "c")


def _members(axes):
    axes = axes if isinstance(axes, tuple) else (axes,)
    n = 1
    for a in axes:
        n *= lax.axis_size(a)
    return n


def _all_gather_a2a(x, axes):
    n = _members(axes)
    copies = jnp.broadcast_to(x[None], (n,) + x.shape)
    out = lax.all_to_all(copies, axes, 0, 0, tiled=True)
    return out.reshape((n * x.shape[0],) + x.shape[1:])


def _reduce_scatter_a2a(x, axes):
    n = _members(axes)
    rows, cols = x.shape
    blocks = x.reshape(rows, n, cols // n).transpose(1, 0, 2)
    return jnp.sum(lax.all_to_all(blocks, axes, 0, 0, tiled=True), axis=0)


def _all_reduce_a2a(x, axes):
    n = _members(axes)
    copies = jnp.broadcast_to(x[None], (n,) + x.shape)
    return jnp.sum(lax.all_to_all(copies, axes, 0, 0, tiled=True), axis=0)


def _shift(v, axis, n, k):
    return lax.ppermute(v, axis, [(i, (i + k) % n) for i in range(n)])


def _pair_reduce_scatter(x, axis, dim):
    lo, hi = jnp.split(x, 2, axis=dim)
    first = lax.axis_index(axis) == 0
    keep = jnp.where(first, lo, hi)
    send = jnp.where(first, hi, lo)
    return keep + lax.ppermute(send, axis, [(0, 1), (1, 0)])


def _ring_gather_matmul(x, weight, axis, n):
    me = lax.axis_index(axis)
    rows = weight.shape[0] // n

    def term(v, owner):
        w = lax.dynamic_slice_in_dim(weight, (owner % n) * rows, rows, axis=0)
        return jnp.dot(v, w, preferred_element_type=jnp.float32)

    total = term(x, me)
    cur_f = cur_b = x
    n_f = n // 2
    n_b = n - 1 - n_f
    for step in range(max(n_f, n_b)):
        if step < n_f:
            cur_f = _shift(cur_f, axis, n, 1)
            total = total + term(cur_f, me - 1 - step)
        if step < n_b:
            cur_b = _shift(cur_b, axis, n, -1)
            total = total + term(cur_b, me + 1 + step)
    return total


def local(hidden, head_weight, lengths, pairing):
    half = NSEQ // 2
    near = ("zl", "yl", "c")
    gathered = _all_gather_a2a(hidden, "zh")
    n_zh = lax.axis_size("zh")
    gathered = _all_gather_a2a(gathered, near)
    gathered = gathered.reshape(_members(near), n_zh, hidden.shape[0], hidden.shape[1])
    gathered = gathered.transpose(1, 0, 2, 3).reshape(-1, hidden.shape[1])
    total_rows = gathered.shape[0]
    seq_len = total_rows // NSEQ
    n_x = lax.axis_size("x")
    partial_logits = lax.dot_general(
        gathered,
        head_weight,
        (((1,), (1,)), ((), ())),
        preferred_element_type=jnp.float32,
    )
    logits = _reduce_scatter_a2a(partial_logits, SEC)
    columns = logits.shape[1]
    soft = jax.nn.softplus(logits)
    act = jnp.log1p(soft)
    positions = jnp.arange(seq_len, dtype=jnp.int32)
    live = (positions[None, :] < lengths[:, None]).astype(jnp.float32)
    expo = jnp.exp(act / pool_temp).reshape(NSEQ, seq_len, columns) * live[:, :, None]
    totals = jnp.sum(expo, axis=1)
    pooled = pool_temp * jnp.log(totals)
    queries = pooled[:half]
    documents = pooled[half:]
    dots_part = lax.dot_general(
        queries, documents, (((1,), (1,)), ((), ())), precision=lax.Precision.HIGHEST
    )
    norms_part = jnp.sum(pooled * pooled, axis=1)
    stats = jnp.concatenate([dots_part.reshape(-1), norms_part])
    for axes in (VOC, SEC):
        stats = _all_reduce_a2a(stats, axes)
    dots = stats[: half * half].reshape(half, half)
    norms = stats[half * half :]
    inv = lax.rsqrt(norms + eps_norm)
    inv_q = inv[:half]
    inv_d = inv[half:]
    scores = dots * inv_q[:, None] * inv_d[None, :] / score_temp
    weights = jnp.exp(scores)
    row_sum = jnp.sum(weights, axis=1)
    probs = weights / row_sum[:, None]
    target = (jnp.arange(half, dtype=jnp.int32)[None, :] == pairing[:, None]).astype(jnp.float32)
    loss = jnp.sum(jnp.log(row_sum) - jnp.sum(scores * target, axis=1))
    dscore = grad_scale * (probs - target)
    gdots = dscore * inv_q[:, None] * inv_d[None, :] / score_temp
    dinv_q = jnp.sum(dscore * dots * inv_d[None, :], axis=1) / score_temp
    dinv_d = jnp.sum(dscore * dots * inv_q[:, None], axis=0) / score_temp
    dinv = jnp.concatenate([dinv_q, dinv_d])
    dnorm = -0.5 * dinv * inv * inv * inv
    dpool_q = (
        jnp.dot(gdots, documents, precision=lax.Precision.HIGHEST)
        + 2.0 * dnorm[:half, None] * queries
    )
    dpool_d = (
        jnp.dot(gdots.T, queries, precision=lax.Precision.HIGHEST)
        + 2.0 * dnorm[half:, None] * documents
    )
    dpooled = jnp.concatenate([dpool_q, dpool_d], axis=0)
    dact = (dpooled[:, None, :] * expo / totals[:, None, :]).reshape(total_rows, columns)
    dlogit = (dact * jax.nn.sigmoid(logits) / (1.0 + soft)).astype(jnp.bfloat16)
    n_sec = _members(SEC)
    dlogit = _all_gather_a2a(dlogit[None], SEC)
    weight = head_weight.reshape(n_sec, columns, head_weight.shape[1])
    partial_grad = lax.dot_general(
        dlogit, weight, (((0, 2), (0, 1)), ((), ())), preferred_element_type=jnp.float32
    )
    n_near = _members(near)
    rows = hidden.shape[0]
    grad = partial_grad.reshape(n_zh, n_near, rows, partial_grad.shape[1]).transpose(1, 0, 2, 3)
    grad = jnp.sum(lax.all_to_all(grad, near, 0, 0, tiled=True), axis=0)
    hidden_grad = jnp.sum(lax.all_to_all(grad, "zh", 0, 0, tiled=True), axis=0)
    return (hidden_grad, loss)


def solution(mesh):
    n_sec, n_voc = mesh.devices.shape
    fine = Mesh(
        mesh.devices.reshape(n_sec // 2, 2, n_voc // 16, 4, 2, 2), SEC + VOC
    )
    in_specs = (P(VOC, SEC), P(VOC, SEC), P(), P())
    out_specs = (P(VOC, SEC), P())
    return jax.shard_map(local, mesh=fine, in_specs=in_specs, out_specs=out_specs, check_vma=False)
```

```python
import jax
import jax.numpy as jnp
from jax import lax
from jax.sharding import Mesh
from jax.sharding import PartitionSpec as P

NSEQ = 8


pool_temp = 0.5
score_temp = 0.02
grad_scale = 16.0
eps_norm = 1e-06

SEC = ("x", "yh")
Z = ("zh", "zl")
VOC = Z + ("yl", "c")


def _members(axes):
    axes = axes if isinstance(axes, tuple) else (axes,)
    n = 1
    for a in axes:
        n *= lax.axis_size(a)
    return n


def _all_gather_a2a(x, axes):
    n = _members(axes)
    copies = jnp.broadcast_to(x[None], (n,) + x.shape)
    out = lax.all_to_all(copies, axes, 0, 0, tiled=True)
    return out.reshape((n * x.shape[0],) + x.shape[1:])


def _reduce_scatter_a2a(x, axes):
    n = _members(axes)
    rows, cols = x.shape
    blocks = x.reshape(rows, n, cols // n).transpose(1, 0, 2)
    return jnp.sum(lax.all_to_all(blocks, axes, 0, 0, tiled=True), axis=0)


def _all_reduce_a2a(x, axes):
    n = _members(axes)
    copies = jnp.broadcast_to(x[None], (n,) + x.shape)
    return jnp.sum(lax.all_to_all(copies, axes, 0, 0, tiled=True), axis=0)


def _shift(v, axis, n, k):
    return lax.ppermute(v, axis, [(i, (i + k) % n) for i in range(n)])


def _pair_reduce_scatter(x, axis, dim):
    lo, hi = jnp.split(x, 2, axis=dim)
    first = lax.axis_index(axis) == 0
    keep = jnp.where(first, lo, hi)
    send = jnp.where(first, hi, lo)
    return keep + lax.ppermute(send, axis, [(0, 1), (1, 0)])


def _ring_gather_matmul(x, weight, axis, n):
    me = lax.axis_index(axis)
    rows = weight.shape[0] // n

    def term(v, owner):
        w = lax.dynamic_slice_in_dim(weight, (owner % n) * rows, rows, axis=0)
        return jnp.dot(v, w, preferred_element_type=jnp.float32)

    total = term(x, me)
    cur_f = cur_b = x
    n_f = n // 2
    n_b = n - 1 - n_f
    for step in range(max(n_f, n_b)):
        if step < n_f:
            cur_f = _shift(cur_f, axis, n, 1)
            total = total + term(cur_f, me - 1 - step)
        if step < n_b:
            cur_b = _shift(cur_b, axis, n, -1)
            total = total + term(cur_b, me + 1 + step)
    return total


def local(hidden, head_weight, lengths, pairing):
    half = NSEQ // 2
    near = ("zl", "yl", "c")
    gathered = _all_gather_a2a(hidden, "zh")
    n_zh = lax.axis_size("zh")
    gathered = _all_gather_a2a(gathered, near)
    gathered = gathered.reshape(_members(near), n_zh, hidden.shape[0], hidden.shape[1])
    gathered = gathered.transpose(1, 0, 2, 3).reshape(-1, hidden.shape[1])
    total_rows = gathered.shape[0]
    seq_len = total_rows // NSEQ
    n_x = lax.axis_size("x")
    partial_logits = lax.dot_general(
        gathered,
        head_weight,
        (((1,), (1,)), ((), ())),
        preferred_element_type=jnp.float32,
    )
    logits = _reduce_scatter_a2a(partial_logits, SEC)
    columns = logits.shape[1]
    soft = jax.nn.softplus(logits)
    act = jnp.log1p(soft)
    positions = jnp.arange(seq_len, dtype=jnp.int32)
    live = (positions[None, :] < lengths[:, None]).astype(jnp.float32)
    expo = jnp.exp(act / pool_temp).reshape(NSEQ, seq_len, columns) * live[:, :, None]
    totals = jnp.sum(expo, axis=1)
    pooled = pool_temp * jnp.log(totals)
    queries = pooled[:half]
    documents = pooled[half:]
    dots_part = lax.dot_general(
        queries, documents, (((1,), (1,)), ((), ())), precision=lax.Precision.HIGHEST
    )
    norms_part = jnp.sum(pooled * pooled, axis=1)
    stats = jnp.concatenate([dots_part.reshape(-1), norms_part])
    for axes in (VOC, SEC):
        stats = _all_reduce_a2a(stats, axes)
    dots = stats[: half * half].reshape(half, half)
    norms = stats[half * half :]
    inv = lax.rsqrt(norms + eps_norm)
    inv_q = inv[:half]
    inv_d = inv[half:]
    scores = dots * inv_q[:, None] * inv_d[None, :] / score_temp
    weights = jnp.exp(scores)
    row_sum = jnp.sum(weights, axis=1)
    probs = weights / row_sum[:, None]
    target = (jnp.arange(half, dtype=jnp.int32)[None, :] == pairing[:, None]).astype(jnp.float32)
    loss = jnp.sum(jnp.log(row_sum) - jnp.sum(scores * target, axis=1))
    dscore = grad_scale * (probs - target)
    gdots = dscore * inv_q[:, None] * inv_d[None, :] / score_temp
    dinv_q = jnp.sum(dscore * dots * inv_d[None, :], axis=1) / score_temp
    dinv_d = jnp.sum(dscore * dots * inv_q[:, None], axis=0) / score_temp
    dinv = jnp.concatenate([dinv_q, dinv_d])
    dnorm = -0.5 * dinv * inv * inv * inv
    dpool_q = (
        jnp.dot(gdots, documents, precision=lax.Precision.HIGHEST)
        + 2.0 * dnorm[:half, None] * queries
    )
    dpool_d = (
        jnp.dot(gdots.T, queries, precision=lax.Precision.HIGHEST)
        + 2.0 * dnorm[half:, None] * documents
    )
    dpooled = jnp.concatenate([dpool_q, dpool_d], axis=0)
    dact = (dpooled[:, None, :] * expo / totals[:, None, :]).reshape(total_rows, columns)
    dlogit = (dact * jax.nn.sigmoid(logits) / (1.0 + soft)).astype(jnp.bfloat16)
    n_sec = _members(SEC)
    dlogit = _all_gather_a2a(dlogit[None], SEC)
    weight = head_weight.reshape(n_sec, columns, head_weight.shape[1])
    partial_grad = lax.dot_general(
        dlogit, weight, (((0, 2), (0, 1)), ((), ())), preferred_element_type=jnp.float32
    )
    n_zl, n_yl, n_c = (lax.axis_size(a) for a in near)
    rows = hidden.shape[0]
    width = partial_grad.shape[1]
    grad = partial_grad.reshape(n_zh, n_zl, n_yl, n_c, rows, width).transpose(3, 0, 1, 2, 4, 5)
    grad = jnp.sum(lax.all_to_all(grad, "c", 0, 0, tiled=True), axis=0)
    grad = grad.transpose(1, 2, 0, 3, 4).reshape(n_zl * n_yl, n_zh, rows, width)
    grad = jnp.sum(lax.all_to_all(grad, ("zl", "yl"), 0, 0, tiled=True), axis=0)
    hidden_grad = jnp.sum(lax.all_to_all(grad, "zh", 0, 0, tiled=True), axis=0)
    return (hidden_grad, loss)


def solution(mesh):
    n_sec, n_voc = mesh.devices.shape
    fine = Mesh(
        mesh.devices.reshape(n_sec // 2, 2, n_voc // 16, 4, 2, 2), SEC + VOC
    )
    in_specs = (P(VOC, SEC), P(VOC, SEC), P(), P())
    out_specs = (P(VOC, SEC), P())
    return jax.shard_map(local, mesh=fine, in_specs=in_specs, out_specs=out_specs, check_vma=False)
```

```python
import jax
import jax.numpy as jnp
from jax import lax
from jax.sharding import Mesh
from jax.sharding import PartitionSpec as P

NSEQ = 8


pool_temp = 0.5
score_temp = 0.02
grad_scale = 16.0
eps_norm = 1e-06

SEC = ("x", "yh")
Z = ("zh", "zl")
VOC = Z + ("yl", "c")


def _members(axes):
    axes = axes if isinstance(axes, tuple) else (axes,)
    n = 1
    for a in axes:
        n *= lax.axis_size(a)
    return n


def _all_gather_a2a(x, axes):
    n = _members(axes)
    copies = jnp.broadcast_to(x[None], (n,) + x.shape)
    out = lax.all_to_all(copies, axes, 0, 0, tiled=True)
    return out.reshape((n * x.shape[0],) + x.shape[1:])


def _copies_a2a(x, axes):
    n = _members(axes)
    return lax.all_to_all(jnp.broadcast_to(x[None], (n,) + x.shape), axes, 0, 0, tiled=True)


def _reduce_scatter_a2a(x, axes):
    n = _members(axes)
    rows, cols = x.shape
    blocks = x.reshape(rows, n, cols // n).transpose(1, 0, 2)
    return jnp.sum(lax.all_to_all(blocks, axes, 0, 0, tiled=True), axis=0)


def _all_reduce_a2a(x, axes):
    n = _members(axes)
    copies = jnp.broadcast_to(x[None], (n,) + x.shape)
    return jnp.sum(lax.all_to_all(copies, axes, 0, 0, tiled=True), axis=0)


def _shift(v, axis, n, k):
    return lax.ppermute(v, axis, [(i, (i + k) % n) for i in range(n)])


def _pair_reduce_scatter(x, axis, dim):
    lo, hi = jnp.split(x, 2, axis=dim)
    first = lax.axis_index(axis) == 0
    keep = jnp.where(first, lo, hi)
    send = jnp.where(first, hi, lo)
    return keep + lax.ppermute(send, axis, [(0, 1), (1, 0)])


def _ring_gather_matmul(x, weight, axis, n):
    me = lax.axis_index(axis)
    rows = weight.shape[0] // n

    def term(v, owner):
        w = lax.dynamic_slice_in_dim(weight, (owner % n) * rows, rows, axis=0)
        return jnp.dot(v, w, preferred_element_type=jnp.float32)

    total = term(x, me)
    cur_f = cur_b = x
    n_f = n // 2
    n_b = n - 1 - n_f
    for step in range(max(n_f, n_b)):
        if step < n_f:
            cur_f = _shift(cur_f, axis, n, 1)
            total = total + term(cur_f, me - 1 - step)
        if step < n_b:
            cur_b = _shift(cur_b, axis, n, -1)
            total = total + term(cur_b, me + 1 + step)
    return total


def local(hidden, head_weight, lengths, pairing):
    half = NSEQ // 2
    near = ("zl", "yl", "c")
    n_zh = lax.axis_size("zh")
    gathered = _copies_a2a(hidden, "zh")
    gathered = _copies_a2a(gathered, ("zl", "yl"))
    gathered = _copies_a2a(gathered, "c")
    gathered = gathered.transpose(2, 1, 0, 3, 4).reshape(-1, hidden.shape[1])
    total_rows = gathered.shape[0]
    seq_len = total_rows // NSEQ
    n_x = lax.axis_size("x")
    partial_logits = lax.dot_general(
        gathered,
        head_weight,
        (((1,), (1,)), ((), ())),
        preferred_element_type=jnp.float32,
    )
    logits = _reduce_scatter_a2a(partial_logits, SEC)
    columns = logits.shape[1]
    soft = jax.nn.softplus(logits)
    act = jnp.log1p(soft)
    positions = jnp.arange(seq_len, dtype=jnp.int32)
    live = (positions[None, :] < lengths[:, None]).astype(jnp.float32)
    expo = jnp.exp(act / pool_temp).reshape(NSEQ, seq_len, columns) * live[:, :, None]
    totals = jnp.sum(expo, axis=1)
    pooled = pool_temp * jnp.log(totals)
    queries = pooled[:half]
    documents = pooled[half:]
    dots_part = lax.dot_general(
        queries, documents, (((1,), (1,)), ((), ())), precision=lax.Precision.HIGHEST
    )
    norms_part = jnp.sum(pooled * pooled, axis=1)
    stats = jnp.concatenate([dots_part.reshape(-1), norms_part])
    for axes in (VOC, SEC):
        stats = _all_reduce_a2a(stats, axes)
    dots = stats[: half * half].reshape(half, half)
    norms = stats[half * half :]
    inv = lax.rsqrt(norms + eps_norm)
    inv_q = inv[:half]
    inv_d = inv[half:]
    scores = dots * inv_q[:, None] * inv_d[None, :] / score_temp
    weights = jnp.exp(scores)
    row_sum = jnp.sum(weights, axis=1)
    probs = weights / row_sum[:, None]
    target = (jnp.arange(half, dtype=jnp.int32)[None, :] == pairing[:, None]).astype(jnp.float32)
    loss = jnp.sum(jnp.log(row_sum) - jnp.sum(scores * target, axis=1))
    dscore = grad_scale * (probs - target)
    gdots = dscore * inv_q[:, None] * inv_d[None, :] / score_temp
    dinv_q = jnp.sum(dscore * dots * inv_d[None, :], axis=1) / score_temp
    dinv_d = jnp.sum(dscore * dots * inv_q[:, None], axis=0) / score_temp
    dinv = jnp.concatenate([dinv_q, dinv_d])
    dnorm = -0.5 * dinv * inv * inv * inv
    dpool_q = (
        jnp.dot(gdots, documents, precision=lax.Precision.HIGHEST)
        + 2.0 * dnorm[:half, None] * queries
    )
    dpool_d = (
        jnp.dot(gdots.T, queries, precision=lax.Precision.HIGHEST)
        + 2.0 * dnorm[half:, None] * documents
    )
    dpooled = jnp.concatenate([dpool_q, dpool_d], axis=0)
    dact = (dpooled[:, None, :] * expo / totals[:, None, :]).reshape(total_rows, columns)
    dlogit = (dact * jax.nn.sigmoid(logits) / (1.0 + soft)).astype(jnp.bfloat16)
    n_sec = _members(SEC)
    dlogit = _all_gather_a2a(dlogit[None], SEC)
    weight = head_weight.reshape(n_sec, columns, head_weight.shape[1])
    partial_grad = lax.dot_general(
        dlogit, weight, (((0, 2), (0, 1)), ((), ())), preferred_element_type=jnp.float32
    )
    n_zl, n_yl, n_c = (lax.axis_size(a) for a in near)
    rows = hidden.shape[0]
    width = partial_grad.shape[1]
    grad = partial_grad.reshape(n_zh, n_zl, n_yl, n_c, rows, width).transpose(3, 0, 1, 2, 4, 5)
    grad = jnp.sum(lax.all_to_all(grad, "c", 0, 0, tiled=True), axis=0)
    grad = grad.transpose(1, 2, 0, 3, 4).reshape(n_zl * n_yl, n_zh, rows, width)
    grad = jnp.sum(lax.all_to_all(grad, ("zl", "yl"), 0, 0, tiled=True), axis=0)
    hidden_grad = jnp.sum(lax.all_to_all(grad, "zh", 0, 0, tiled=True), axis=0)
    return (hidden_grad, loss)


def solution(mesh):
    n_sec, n_voc = mesh.devices.shape
    fine = Mesh(
        mesh.devices.reshape(n_sec // 2, 2, n_voc // 16, 4, 2, 2), SEC + VOC
    )
    in_specs = (P(VOC, SEC), P(VOC, SEC), P(), P())
    out_specs = (P(VOC, SEC), P())
    return jax.shard_map(local, mesh=fine, in_specs=in_specs, out_specs=out_specs, check_vma=False)
```

```python
import jax
import jax.numpy as jnp
from jax import lax
from jax.experimental.layout import Layout, with_layout_constraint
from jax.sharding import Mesh
from jax.sharding import PartitionSpec as P

NSEQ = 8


pool_temp = 0.5
score_temp = 0.02
grad_scale = 16.0
eps_norm = 1e-06

SEC = ("x", "yh")
Z = ("zh", "zl")
VOC = Z + ("yl", "c")


def _members(axes):
    axes = axes if isinstance(axes, tuple) else (axes,)
    n = 1
    for a in axes:
        n *= lax.axis_size(a)
    return n


def _all_gather_a2a(x, axes):
    n = _members(axes)
    copies = jnp.broadcast_to(x[None], (n,) + x.shape)
    out = lax.all_to_all(copies, axes, 0, 0, tiled=True)
    return out.reshape((n * x.shape[0],) + x.shape[1:])


def _copies_a2a(x, axes):
    n = _members(axes)
    return lax.all_to_all(jnp.broadcast_to(x[None], (n,) + x.shape), axes, 0, 0, tiled=True)


def _reduce_scatter_a2a(x, axes):
    n = _members(axes)
    rows, cols = x.shape
    blocks = x.reshape(rows, n, cols // n).transpose(1, 0, 2)
    return jnp.sum(lax.all_to_all(blocks, axes, 0, 0, tiled=True), axis=0)


def _all_reduce_a2a(x, axes):
    n = _members(axes)
    copies = jnp.broadcast_to(x[None], (n,) + x.shape)
    return jnp.sum(lax.all_to_all(copies, axes, 0, 0, tiled=True), axis=0)


def _shift(v, axis, n, k):
    return lax.ppermute(v, axis, [(i, (i + k) % n) for i in range(n)])


def _pair_reduce_scatter(x, axis, dim):
    lo, hi = jnp.split(x, 2, axis=dim)
    first = lax.axis_index(axis) == 0
    keep = jnp.where(first, lo, hi)
    send = jnp.where(first, hi, lo)
    return keep + lax.ppermute(send, axis, [(0, 1), (1, 0)])


def _ring_gather_matmul(x, weight, axis, n):
    me = lax.axis_index(axis)
    rows = weight.shape[0] // n

    def term(v, owner):
        w = lax.dynamic_slice_in_dim(weight, (owner % n) * rows, rows, axis=0)
        return jnp.dot(v, w, preferred_element_type=jnp.float32)

    total = term(x, me)
    cur_f = cur_b = x
    n_f = n // 2
    n_b = n - 1 - n_f
    for step in range(max(n_f, n_b)):
        if step < n_f:
            cur_f = _shift(cur_f, axis, n, 1)
            total = total + term(cur_f, me - 1 - step)
        if step < n_b:
            cur_b = _shift(cur_b, axis, n, -1)
            total = total + term(cur_b, me + 1 + step)
    return total


def local(hidden, head_weight, lengths, pairing):
    half = NSEQ // 2
    near = ("zl", "yl", "c")
    n_zh = lax.axis_size("zh")
    gathered = _copies_a2a(hidden, "zh")
    gathered = _copies_a2a(gathered, ("zl", "yl"))
    gathered = _copies_a2a(gathered, "c")
    gathered = gathered.transpose(2, 1, 0, 3, 4).reshape(-1, hidden.shape[1])
    total_rows = gathered.shape[0]
    seq_len = total_rows // NSEQ
    n_x = lax.axis_size("x")
    partial_logits = lax.dot_general(
        gathered,
        head_weight,
        (((1,), (1,)), ((), ())),
        preferred_element_type=jnp.float32,
    )
    logits = _reduce_scatter_a2a(partial_logits, SEC)
    logits = with_layout_constraint(logits, Layout((0, 1)))
    columns = logits.shape[1]
    soft = jax.nn.softplus(logits)
    act = jnp.log1p(soft)
    positions = jnp.arange(seq_len, dtype=jnp.int32)
    live = (positions[None, :] < lengths[:, None]).astype(jnp.float32)
    expo = jnp.exp(act / pool_temp).reshape(NSEQ, seq_len, columns) * live[:, :, None]
    totals = jnp.sum(expo, axis=1)
    pooled = pool_temp * jnp.log(totals)
    queries = pooled[:half]
    documents = pooled[half:]
    dots_part = lax.dot_general(
        queries, documents, (((1,), (1,)), ((), ())), precision=lax.Precision.HIGHEST
    )
    norms_part = jnp.sum(pooled * pooled, axis=1)
    stats = jnp.concatenate([dots_part.reshape(-1), norms_part])
    for axes in (VOC, SEC):
        stats = _all_reduce_a2a(stats, axes)
    dots = stats[: half * half].reshape(half, half)
    norms = stats[half * half :]
    inv = lax.rsqrt(norms + eps_norm)
    inv_q = inv[:half]
    inv_d = inv[half:]
    scores = dots * inv_q[:, None] * inv_d[None, :] / score_temp
    weights = jnp.exp(scores)
    row_sum = jnp.sum(weights, axis=1)
    probs = weights / row_sum[:, None]
    target = (jnp.arange(half, dtype=jnp.int32)[None, :] == pairing[:, None]).astype(jnp.float32)
    loss = jnp.sum(jnp.log(row_sum) - jnp.sum(scores * target, axis=1))
    dscore = grad_scale * (probs - target)
    gdots = dscore * inv_q[:, None] * inv_d[None, :] / score_temp
    dinv_q = jnp.sum(dscore * dots * inv_d[None, :], axis=1) / score_temp
    dinv_d = jnp.sum(dscore * dots * inv_q[:, None], axis=0) / score_temp
    dinv = jnp.concatenate([dinv_q, dinv_d])
    dnorm = -0.5 * dinv * inv * inv * inv
    dpool_q = (
        jnp.dot(gdots, documents, precision=lax.Precision.HIGHEST)
        + 2.0 * dnorm[:half, None] * queries
    )
    dpool_d = (
        jnp.dot(gdots.T, queries, precision=lax.Precision.HIGHEST)
        + 2.0 * dnorm[half:, None] * documents
    )
    dpooled = jnp.concatenate([dpool_q, dpool_d], axis=0)
    dact = (dpooled[:, None, :] * expo / totals[:, None, :]).reshape(total_rows, columns)
    dlogit = (dact * jax.nn.sigmoid(logits) / (1.0 + soft)).astype(jnp.bfloat16)
    dlogit = with_layout_constraint(dlogit, Layout((0, 1)))
    n_sec = _members(SEC)
    dlogit = _all_gather_a2a(dlogit[None], SEC)
    weight = head_weight.reshape(n_sec, columns, head_weight.shape[1])
    partial_grad = lax.dot_general(
        dlogit, weight, (((0, 2), (0, 1)), ((), ())), preferred_element_type=jnp.float32
    )
    n_zl, n_yl, n_c = (lax.axis_size(a) for a in near)
    rows = hidden.shape[0]
    width = partial_grad.shape[1]
    grad = partial_grad.reshape(n_zh, n_zl, n_yl, n_c, rows, width).transpose(3, 0, 1, 2, 4, 5)
    grad = jnp.sum(lax.all_to_all(grad, "c", 0, 0, tiled=True), axis=0)
    grad = grad.transpose(1, 2, 0, 3, 4).reshape(n_zl * n_yl, n_zh, rows, width)
    grad = jnp.sum(lax.all_to_all(grad, ("zl", "yl"), 0, 0, tiled=True), axis=0)
    hidden_grad = jnp.sum(lax.all_to_all(grad, "zh", 0, 0, tiled=True), axis=0)
    return (hidden_grad, loss)


def solution(mesh):
    n_sec, n_voc = mesh.devices.shape
    fine = Mesh(
        mesh.devices.reshape(n_sec // 2, 2, n_voc // 16, 4, 2, 2), SEC + VOC
    )
    in_specs = (P(VOC, SEC), P(VOC, SEC), P(), P())
    out_specs = (P(VOC, SEC), P())
    return jax.shard_map(local, mesh=fine, in_specs=in_specs, out_specs=out_specs, check_vma=False)
```

```python
import jax
import jax.numpy as jnp
from jax import lax
from jax.experimental.layout import Layout, with_layout_constraint
from jax.sharding import Mesh
from jax.sharding import PartitionSpec as P

NSEQ = 8


pool_temp = 0.5
score_temp = 0.02
grad_scale = 16.0
eps_norm = 1e-06

SEC = ("x", "yh")
Z = ("zh", "zl")
VOC = Z + ("yl", "c")


def _members(axes):
    axes = axes if isinstance(axes, tuple) else (axes,)
    n = 1
    for a in axes:
        n *= lax.axis_size(a)
    return n


def _all_gather_a2a(x, axes):
    n = _members(axes)
    copies = jnp.broadcast_to(x[None], (n,) + x.shape)
    out = lax.all_to_all(copies, axes, 0, 0, tiled=True)
    return out.reshape((n * x.shape[0],) + x.shape[1:])


def _copies_a2a(x, axes):
    n = _members(axes)
    return lax.all_to_all(jnp.broadcast_to(x[None], (n,) + x.shape), axes, 0, 0, tiled=True)


def _reduce_scatter_a2a(x, axes):
    n = _members(axes)
    rows, cols = x.shape
    blocks = x.reshape(rows, n, cols // n).transpose(1, 0, 2)
    return jnp.sum(lax.all_to_all(blocks, axes, 0, 0, tiled=True), axis=0)


def _all_reduce_a2a(x, axes):
    n = _members(axes)
    copies = jnp.broadcast_to(x[None], (n,) + x.shape)
    return jnp.sum(lax.all_to_all(copies, axes, 0, 0, tiled=True), axis=0)


def _shift(v, axis, n, k):
    return lax.ppermute(v, axis, [(i, (i + k) % n) for i in range(n)])


def _pair_reduce_scatter(x, axis, dim):
    lo, hi = jnp.split(x, 2, axis=dim)
    first = lax.axis_index(axis) == 0
    keep = jnp.where(first, lo, hi)
    send = jnp.where(first, hi, lo)
    return keep + lax.ppermute(send, axis, [(0, 1), (1, 0)])


def _ring_gather_matmul(x, weight, axis, n):
    me = lax.axis_index(axis)
    rows = weight.shape[0] // n

    def term(v, owner):
        w = lax.dynamic_slice_in_dim(weight, (owner % n) * rows, rows, axis=0)
        return jnp.dot(v, w, preferred_element_type=jnp.float32)

    total = term(x, me)
    cur_f = cur_b = x
    n_f = n // 2
    n_b = n - 1 - n_f
    for step in range(max(n_f, n_b)):
        if step < n_f:
            cur_f = _shift(cur_f, axis, n, 1)
            total = total + term(cur_f, me - 1 - step)
        if step < n_b:
            cur_b = _shift(cur_b, axis, n, -1)
            total = total + term(cur_b, me + 1 + step)
    return total


def local(hidden, head_weight, lengths, pairing):
    half = NSEQ // 2
    near = ("zl", "yl", "c")
    n_zh = lax.axis_size("zh")
    gathered = _copies_a2a(hidden, "zh")
    gathered = _copies_a2a(gathered, ("zl", "yl"))
    gathered = _copies_a2a(gathered, "c")
    gathered = gathered.transpose(2, 1, 0, 3, 4).reshape(-1, hidden.shape[1])
    total_rows = gathered.shape[0]
    seq_len = total_rows // NSEQ
    n_x = lax.axis_size("x")
    partial_logits = lax.dot_general(
        gathered,
        head_weight,
        (((1,), (1,)), ((), ())),
        preferred_element_type=jnp.float32,
    )
    logits = _reduce_scatter_a2a(partial_logits, SEC)
    logits = with_layout_constraint(logits, Layout((0, 1)))
    columns = logits.shape[1]
    soft = jax.nn.softplus(logits)
    act = jnp.log1p(soft)
    positions = jnp.arange(seq_len, dtype=jnp.int32)
    live = (positions[None, :] < lengths[:, None]).astype(jnp.float32)
    expo = jnp.exp(act / pool_temp).reshape(NSEQ, seq_len, columns) * live[:, :, None]
    totals = jnp.sum(expo, axis=1)
    pooled = pool_temp * jnp.log(totals)
    queries = pooled[:half]
    documents = pooled[half:]
    dots_part = lax.dot_general(
        queries, documents, (((1,), (1,)), ((), ())), precision=lax.Precision.HIGHEST
    )
    norms_part = jnp.sum(pooled * pooled, axis=1)
    stats = jnp.concatenate([dots_part.reshape(-1), norms_part])
    for axes in (VOC, SEC):
        stats = _all_reduce_a2a(stats, axes)
    dots = stats[: half * half].reshape(half, half)
    norms = stats[half * half :]
    inv = lax.rsqrt(norms + eps_norm)
    inv_q = inv[:half]
    inv_d = inv[half:]
    scores = dots * inv_q[:, None] * inv_d[None, :] / score_temp
    weights = jnp.exp(scores)
    row_sum = jnp.sum(weights, axis=1)
    probs = weights / row_sum[:, None]
    target = (jnp.arange(half, dtype=jnp.int32)[None, :] == pairing[:, None]).astype(jnp.float32)
    loss = jnp.sum(jnp.log(row_sum) - jnp.sum(scores * target, axis=1))
    dscore = grad_scale * (probs - target)
    gdots = dscore * inv_q[:, None] * inv_d[None, :] / score_temp
    dinv_q = jnp.sum(dscore * dots * inv_d[None, :], axis=1) / score_temp
    dinv_d = jnp.sum(dscore * dots * inv_q[:, None], axis=0) / score_temp
    dinv = jnp.concatenate([dinv_q, dinv_d])
    dnorm = -0.5 * dinv * inv * inv * inv
    dpool_q = (
        jnp.dot(gdots, documents, precision=lax.Precision.HIGHEST)
        + 2.0 * dnorm[:half, None] * queries
    )
    dpool_d = (
        jnp.dot(gdots.T, queries, precision=lax.Precision.HIGHEST)
        + 2.0 * dnorm[half:, None] * documents
    )
    dpooled = jnp.concatenate([dpool_q, dpool_d], axis=0)
    dact = (dpooled[:, None, :] * expo / totals[:, None, :]).reshape(total_rows, columns)
    dlogit = (dact * jax.nn.sigmoid(logits) / (1.0 + soft)).astype(jnp.bfloat16)
    dlogit = with_layout_constraint(dlogit, Layout((0, 1)))
    n_sec = _members(SEC)
    copies = jnp.broadcast_to(dlogit.T[None], (n_sec,) + dlogit.T.shape)
    copies = with_layout_constraint(copies, Layout((0, 1, 2)))
    dlogit_t = lax.all_to_all(copies, SEC, 0, 0, tiled=True).reshape(-1, dlogit.shape[0])
    grad_t = lax.dot_general(
        head_weight, dlogit_t, (((0,), (0,)), ((), ())), preferred_element_type=jnp.float32
    )
    n_zl, n_yl, n_c = (lax.axis_size(a) for a in near)
    rows = hidden.shape[0]
    width = grad_t.shape[0]
    grad = grad_t.reshape(width, n_zh, n_zl, n_yl, n_c, rows).transpose(4, 1, 2, 3, 0, 5)
    grad = jnp.sum(lax.all_to_all(grad, "c", 0, 0, tiled=True), axis=0)
    grad = grad.transpose(1, 2, 0, 3, 4).reshape(n_zl * n_yl, n_zh, width, rows)
    grad = jnp.sum(lax.all_to_all(grad, ("zl", "yl"), 0, 0, tiled=True), axis=0)
    hidden_grad = jnp.sum(lax.all_to_all(grad, "zh", 0, 0, tiled=True), axis=0).T
    return (hidden_grad, loss)


def solution(mesh):
    n_sec, n_voc = mesh.devices.shape
    fine = Mesh(
        mesh.devices.reshape(n_sec // 2, 2, n_voc // 16, 4, 2, 2), SEC + VOC
    )
    in_specs = (P(VOC, SEC), P(VOC, SEC), P(), P())
    out_specs = (P(VOC, SEC), P())
    return jax.shard_map(local, mesh=fine, in_specs=in_specs, out_specs=out_specs, check_vma=False)
```

```python
import jax
import jax.numpy as jnp
from jax import lax
from jax.experimental.layout import Layout, with_layout_constraint
from jax.sharding import Mesh
from jax.sharding import PartitionSpec as P

NSEQ = 8


pool_temp = 0.5
score_temp = 0.02
grad_scale = 16.0
eps_norm = 1e-06

SEC = ("x", "yh")
Z = ("zh", "zl")
VOC = Z + ("yl", "c")


def _members(axes):
    axes = axes if isinstance(axes, tuple) else (axes,)
    n = 1
    for a in axes:
        n *= lax.axis_size(a)
    return n


def _all_gather_a2a(x, axes):
    n = _members(axes)
    copies = jnp.broadcast_to(x[None], (n,) + x.shape)
    out = lax.all_to_all(copies, axes, 0, 0, tiled=True)
    return out.reshape((n * x.shape[0],) + x.shape[1:])


def _copies_a2a(x, axes):
    n = _members(axes)
    return lax.all_to_all(jnp.broadcast_to(x[None], (n,) + x.shape), axes, 0, 0, tiled=True)


def _reduce_scatter_a2a(x, axes):
    n = _members(axes)
    rows, cols = x.shape
    blocks = x.reshape(rows, n, cols // n).transpose(1, 0, 2)
    return jnp.sum(lax.all_to_all(blocks, axes, 0, 0, tiled=True), axis=0)


def _all_reduce_a2a(x, axes):
    n = _members(axes)
    copies = jnp.broadcast_to(x[None], (n,) + x.shape)
    return jnp.sum(lax.all_to_all(copies, axes, 0, 0, tiled=True), axis=0)


def _shift(v, axis, n, k):
    return lax.ppermute(v, axis, [(i, (i + k) % n) for i in range(n)])


def _pair_reduce_scatter(x, axis, dim):
    lo, hi = jnp.split(x, 2, axis=dim)
    first = lax.axis_index(axis) == 0
    keep = jnp.where(first, lo, hi)
    send = jnp.where(first, hi, lo)
    return keep + lax.ppermute(send, axis, [(0, 1), (1, 0)])


def _ring_gather_matmul(x, weight, axis, n):
    me = lax.axis_index(axis)
    rows = weight.shape[0] // n

    def term(v, owner):
        w = lax.dynamic_slice_in_dim(weight, (owner % n) * rows, rows, axis=0)
        return jnp.dot(v, w, preferred_element_type=jnp.float32)

    total = term(x, me)
    cur_f = cur_b = x
    n_f = n // 2
    n_b = n - 1 - n_f
    for step in range(max(n_f, n_b)):
        if step < n_f:
            cur_f = _shift(cur_f, axis, n, 1)
            total = total + term(cur_f, me - 1 - step)
        if step < n_b:
            cur_b = _shift(cur_b, axis, n, -1)
            total = total + term(cur_b, me + 1 + step)
    return total


def local(hidden, head_weight, lengths, pairing):
    half = NSEQ // 2
    near = ("zl", "yl", "c")
    n_zh = lax.axis_size("zh")
    gathered = _copies_a2a(hidden, "zh")
    gathered = _copies_a2a(gathered, ("zl", "yl"))
    gathered = _copies_a2a(gathered, "c")
    gathered = gathered.transpose(2, 1, 0, 3, 4).reshape(-1, hidden.shape[1])
    total_rows = gathered.shape[0]
    seq_len = total_rows // NSEQ
    n_x = lax.axis_size("x")
    partial_logits = lax.dot_general(
        gathered,
        head_weight,
        (((1,), (1,)), ((), ())),
        preferred_element_type=jnp.float32,
    )
    logits = _reduce_scatter_a2a(partial_logits, SEC)
    logits = with_layout_constraint(logits, Layout((0, 1)))
    columns = logits.shape[1]
    soft = jax.nn.softplus(logits)
    act = jnp.log1p(soft)
    positions = jnp.arange(seq_len, dtype=jnp.int32)
    live = (positions[None, :] < lengths[:, None]).astype(jnp.float32)
    expo = jnp.exp(act / pool_temp).reshape(NSEQ, seq_len, columns) * live[:, :, None]
    totals = jnp.sum(expo, axis=1)
    pooled = pool_temp * jnp.log(totals)
    queries = pooled[:half]
    documents = pooled[half:]
    dots_part = lax.dot_general(
        queries, documents, (((1,), (1,)), ((), ())), precision=lax.Precision.HIGHEST
    )
    norms_part = jnp.sum(pooled * pooled, axis=1)
    stats = jnp.concatenate([dots_part.reshape(-1), norms_part])
    for axes in (VOC, SEC):
        stats = _all_reduce_a2a(stats, axes)
    dots = stats[: half * half].reshape(half, half)
    norms = stats[half * half :]
    inv = lax.rsqrt(norms + eps_norm)
    inv_q = inv[:half]
    inv_d = inv[half:]
    scores = dots * inv_q[:, None] * inv_d[None, :] / score_temp
    weights = jnp.exp(scores)
    row_sum = jnp.sum(weights, axis=1)
    probs = weights / row_sum[:, None]
    target = (jnp.arange(half, dtype=jnp.int32)[None, :] == pairing[:, None]).astype(jnp.float32)
    loss = jnp.sum(jnp.log(row_sum) - jnp.sum(scores * target, axis=1))
    dscore = grad_scale * (probs - target)
    gdots = dscore * inv_q[:, None] * inv_d[None, :] / score_temp
    dinv_q = jnp.sum(dscore * dots * inv_d[None, :], axis=1) / score_temp
    dinv_d = jnp.sum(dscore * dots * inv_q[:, None], axis=0) / score_temp
    dinv = jnp.concatenate([dinv_q, dinv_d])
    dnorm = -0.5 * dinv * inv * inv * inv
    dpool_q = (
        jnp.dot(gdots, documents, precision=lax.Precision.HIGHEST)
        + 2.0 * dnorm[:half, None] * queries
    )
    dpool_d = (
        jnp.dot(gdots.T, queries, precision=lax.Precision.HIGHEST)
        + 2.0 * dnorm[half:, None] * documents
    )
    dpooled = jnp.concatenate([dpool_q, dpool_d], axis=0)
    dact = (dpooled[:, None, :] * expo / totals[:, None, :]).reshape(total_rows, columns)
    dlogit = (dact * jax.nn.sigmoid(logits) / (1.0 + soft)).astype(jnp.bfloat16)
    dlogit = with_layout_constraint(dlogit, Layout((0, 1)))
    n_sec = _members(SEC)
    copies = jnp.broadcast_to(dlogit.T[None], (n_sec,) + dlogit.T.shape)
    copies = with_layout_constraint(copies, Layout((0, 1, 2)))
    dlogit_t = lax.all_to_all(copies, SEC, 0, 0, tiled=True).reshape(-1, dlogit.shape[0])
    grad_t = lax.dot_general(
        head_weight, dlogit_t, (((0,), (0,)), ((), ())), preferred_element_type=jnp.float32
    )
    n_zl, n_yl, n_c = (lax.axis_size(a) for a in near)
    rows = hidden.shape[0]
    width = grad_t.shape[0]
    grad = grad_t.reshape(width, n_zh, n_zl, n_yl, n_c, rows).transpose(4, 1, 2, 3, 0, 5)
    grad = jnp.sum(lax.all_to_all(grad, "c", 0, 0, tiled=True), axis=0)
    grad = grad.transpose(2, 0, 1, 3, 4)
    grad = jnp.sum(lax.all_to_all(grad, "yl", 0, 0, tiled=True), axis=0)
    grad = grad.transpose(1, 0, 2, 3)
    grad = jnp.sum(lax.all_to_all(grad, "zl", 0, 0, tiled=True), axis=0)
    hidden_grad = jnp.sum(lax.all_to_all(grad, "zh", 0, 0, tiled=True), axis=0).T
    return (hidden_grad, loss)


def solution(mesh):
    n_sec, n_voc = mesh.devices.shape
    fine = Mesh(
        mesh.devices.reshape(n_sec // 2, 2, n_voc // 16, 4, 2, 2), SEC + VOC
    )
    in_specs = (P(VOC, SEC), P(VOC, SEC), P(), P())
    out_specs = (P(VOC, SEC), P())
    return jax.shard_map(local, mesh=fine, in_specs=in_specs, out_specs=out_specs, check_vma=False)
```

```python
import jax
import jax.numpy as jnp
from jax import lax
from jax.experimental.layout import Layout, with_layout_constraint
from jax.sharding import Mesh
from jax.sharding import PartitionSpec as P

NSEQ = 8


pool_temp = 0.5
score_temp = 0.02
grad_scale = 16.0
eps_norm = 1e-06

SEC = ("x", "yh")
Z = ("zh", "zl")
VOC = Z + ("yl", "c")


def _members(axes):
    axes = axes if isinstance(axes, tuple) else (axes,)
    n = 1
    for a in axes:
        n *= lax.axis_size(a)
    return n


def _all_gather_a2a(x, axes):
    n = _members(axes)
    copies = jnp.broadcast_to(x[None], (n,) + x.shape)
    out = lax.all_to_all(copies, axes, 0, 0, tiled=True)
    return out.reshape((n * x.shape[0],) + x.shape[1:])


def _copies_a2a(x, axes):
    n = _members(axes)
    return lax.all_to_all(jnp.broadcast_to(x[None], (n,) + x.shape), axes, 0, 0, tiled=True)


def _reduce_scatter_a2a(x, axes):
    n = _members(axes)
    rows, cols = x.shape
    blocks = x.reshape(rows, n, cols // n).transpose(1, 0, 2)
    return jnp.sum(lax.all_to_all(blocks, axes, 0, 0, tiled=True), axis=0)


def _all_reduce_a2a(x, axes):
    n = _members(axes)
    copies = jnp.broadcast_to(x[None], (n,) + x.shape)
    return jnp.sum(lax.all_to_all(copies, axes, 0, 0, tiled=True), axis=0)


def _shift(v, axis, n, k):
    return lax.ppermute(v, axis, [(i, (i + k) % n) for i in range(n)])


def _pair_reduce_scatter(x, axis, dim):
    lo, hi = jnp.split(x, 2, axis=dim)
    first = lax.axis_index(axis) == 0
    keep = jnp.where(first, lo, hi)
    send = jnp.where(first, hi, lo)
    return keep + lax.ppermute(send, axis, [(0, 1), (1, 0)])


def _ring_gather_matmul(x, weight, axis, n):
    me = lax.axis_index(axis)
    rows = weight.shape[0] // n

    def term(v, owner):
        w = lax.dynamic_slice_in_dim(weight, (owner % n) * rows, rows, axis=0)
        return jnp.dot(v, w, preferred_element_type=jnp.float32)

    total = term(x, me)
    cur_f = cur_b = x
    n_f = n // 2
    n_b = n - 1 - n_f
    for step in range(max(n_f, n_b)):
        if step < n_f:
            cur_f = _shift(cur_f, axis, n, 1)
            total = total + term(cur_f, me - 1 - step)
        if step < n_b:
            cur_b = _shift(cur_b, axis, n, -1)
            total = total + term(cur_b, me + 1 + step)
    return total


def local(hidden, head_weight, lengths, pairing):
    half = NSEQ // 2
    near = ("zl", "yl", "c")
    n_zh = lax.axis_size("zh")
    gathered = _copies_a2a(hidden, "zh")
    gathered = _copies_a2a(gathered, ("zl", "yl"))
    gathered = _copies_a2a(gathered, "c")
    gathered = gathered.transpose(2, 1, 0, 3, 4).reshape(-1, hidden.shape[1])
    total_rows = gathered.shape[0]
    seq_len = total_rows // NSEQ
    n_x = lax.axis_size("x")
    partial_logits = lax.dot_general(
        gathered,
        head_weight,
        (((1,), (1,)), ((), ())),
        preferred_element_type=jnp.float32,
    )
    logits = _reduce_scatter_a2a(partial_logits, SEC)
    logits = with_layout_constraint(logits, Layout((0, 1)))
    columns = logits.shape[1]
    soft = jax.nn.softplus(logits)
    act = jnp.log1p(soft)
    positions = jnp.arange(seq_len, dtype=jnp.int32)
    live = (positions[None, :] < lengths[:, None]).astype(jnp.float32)
    expo = jnp.exp(act / pool_temp).reshape(NSEQ, seq_len, columns) * live[:, :, None]
    totals = jnp.sum(expo, axis=1)
    pooled = pool_temp * jnp.log(totals)
    queries = pooled[:half]
    documents = pooled[half:]
    dots_part = lax.dot_general(
        queries, documents, (((1,), (1,)), ((), ())), precision=lax.Precision.HIGHEST
    )
    norms_part = jnp.sum(pooled * pooled, axis=1)
    stats = jnp.concatenate([dots_part.reshape(-1), norms_part])
    for axes in (SEC, VOC):
        stats = _all_reduce_a2a(stats, axes)
    dots = stats[: half * half].reshape(half, half)
    norms = stats[half * half :]
    inv = lax.rsqrt(norms + eps_norm)
    inv_q = inv[:half]
    inv_d = inv[half:]
    scores = dots * inv_q[:, None] * inv_d[None, :] / score_temp
    weights = jnp.exp(scores)
    row_sum = jnp.sum(weights, axis=1)
    probs = weights / row_sum[:, None]
    target = (jnp.arange(half, dtype=jnp.int32)[None, :] == pairing[:, None]).astype(jnp.float32)
    loss = jnp.sum(jnp.log(row_sum) - jnp.sum(scores * target, axis=1))
    dscore = grad_scale * (probs - target)
    gdots = dscore * inv_q[:, None] * inv_d[None, :] / score_temp
    dinv_q = jnp.sum(dscore * dots * inv_d[None, :], axis=1) / score_temp
    dinv_d = jnp.sum(dscore * dots * inv_q[:, None], axis=0) / score_temp
    dinv = jnp.concatenate([dinv_q, dinv_d])
    dnorm = -0.5 * dinv * inv * inv * inv
    dpool_q = (
        jnp.dot(gdots, documents, precision=lax.Precision.HIGHEST)
        + 2.0 * dnorm[:half, None] * queries
    )
    dpool_d = (
        jnp.dot(gdots.T, queries, precision=lax.Precision.HIGHEST)
        + 2.0 * dnorm[half:, None] * documents
    )
    dpooled = jnp.concatenate([dpool_q, dpool_d], axis=0)
    dact = (dpooled[:, None, :] * expo / totals[:, None, :]).reshape(total_rows, columns)
    dlogit = (dact * jax.nn.sigmoid(logits) / (1.0 + soft)).astype(jnp.bfloat16)
    dlogit = with_layout_constraint(dlogit, Layout((0, 1)))
    n_sec = _members(SEC)
    copies = jnp.broadcast_to(dlogit.T[None], (n_sec,) + dlogit.T.shape)
    copies = with_layout_constraint(copies, Layout((0, 1, 2)))
    dlogit_t = lax.all_to_all(copies, SEC, 0, 0, tiled=True).reshape(-1, dlogit.shape[0])
    grad_t = lax.dot_general(
        head_weight, dlogit_t, (((0,), (0,)), ((), ())), preferred_element_type=jnp.float32
    )
    n_zl, n_yl, n_c = (lax.axis_size(a) for a in near)
    rows = hidden.shape[0]
    width = grad_t.shape[0]
    grad = grad_t.reshape(width, n_zh, n_zl, n_yl, n_c, rows).transpose(4, 1, 2, 3, 0, 5)
    grad = jnp.sum(lax.all_to_all(grad, "c", 0, 0, tiled=True), axis=0)
    grad = grad.transpose(1, 2, 0, 3, 4).reshape(n_zl * n_yl, n_zh, width, rows)
    grad = jnp.sum(lax.all_to_all(grad, ("zl", "yl"), 0, 0, tiled=True), axis=0)
    hidden_grad = jnp.sum(lax.all_to_all(grad, "zh", 0, 0, tiled=True), axis=0).T
    return (hidden_grad, loss)


def solution(mesh):
    n_sec, n_voc = mesh.devices.shape
    fine = Mesh(
        mesh.devices.reshape(n_sec // 2, 2, n_voc // 16, 4, 2, 2), SEC + VOC
    )
    in_specs = (P(VOC, SEC), P(VOC, SEC), P(), P())
    out_specs = (P(VOC, SEC), P())
    return jax.shard_map(local, mesh=fine, in_specs=in_specs, out_specs=out_specs, check_vma=False)
```

```python
import jax
import jax.numpy as jnp
from jax import lax
from jax.experimental.layout import Layout, with_layout_constraint
from jax.sharding import Mesh
from jax.sharding import PartitionSpec as P

NSEQ = 8


pool_temp = 0.5
score_temp = 0.02
grad_scale = 16.0
eps_norm = 1e-06

SEC = ("x", "yh")
Z = ("zh", "zl")
VOC = Z + ("yl", "c")


def _members(axes):
    axes = axes if isinstance(axes, tuple) else (axes,)
    n = 1
    for a in axes:
        n *= lax.axis_size(a)
    return n


def _all_gather_a2a(x, axes):
    n = _members(axes)
    copies = jnp.broadcast_to(x[None], (n,) + x.shape)
    out = lax.all_to_all(copies, axes, 0, 0, tiled=True)
    return out.reshape((n * x.shape[0],) + x.shape[1:])


def _copies_a2a(x, axes):
    n = _members(axes)
    return lax.all_to_all(jnp.broadcast_to(x[None], (n,) + x.shape), axes, 0, 0, tiled=True)


def _reduce_scatter_a2a(x, axes):
    n = _members(axes)
    rows, cols = x.shape
    blocks = x.reshape(rows, n, cols // n).transpose(1, 0, 2)
    return jnp.sum(lax.all_to_all(blocks, axes, 0, 0, tiled=True), axis=0)


def _all_reduce_a2a(x, axes):
    n = _members(axes)
    copies = jnp.broadcast_to(x[None], (n,) + x.shape)
    return jnp.sum(lax.all_to_all(copies, axes, 0, 0, tiled=True), axis=0)


def _shift(v, axis, n, k):
    return lax.ppermute(v, axis, [(i, (i + k) % n) for i in range(n)])


def _pair_reduce_scatter(x, axis, dim):
    lo, hi = jnp.split(x, 2, axis=dim)
    first = lax.axis_index(axis) == 0
    keep = jnp.where(first, lo, hi)
    send = jnp.where(first, hi, lo)
    return keep + lax.ppermute(send, axis, [(0, 1), (1, 0)])


def _ring_gather_matmul(x, weight, axis, n):
    me = lax.axis_index(axis)
    rows = weight.shape[0] // n

    def term(v, owner):
        w = lax.dynamic_slice_in_dim(weight, (owner % n) * rows, rows, axis=0)
        return jnp.dot(v, w, preferred_element_type=jnp.float32)

    total = term(x, me)
    cur_f = cur_b = x
    n_f = n // 2
    n_b = n - 1 - n_f
    for step in range(max(n_f, n_b)):
        if step < n_f:
            cur_f = _shift(cur_f, axis, n, 1)
            total = total + term(cur_f, me - 1 - step)
        if step < n_b:
            cur_b = _shift(cur_b, axis, n, -1)
            total = total + term(cur_b, me + 1 + step)
    return total


def local(hidden, head_weight, lengths, pairing):
    half = NSEQ // 2
    near = ("zl", "yl", "c")
    n_zh = lax.axis_size("zh")
    gathered = _copies_a2a(hidden, "zh")
    gathered = _copies_a2a(gathered, ("zl", "yl"))
    gathered = _copies_a2a(gathered, "c")
    gathered = gathered.transpose(2, 1, 0, 3, 4).reshape(-1, hidden.shape[1])
    total_rows = gathered.shape[0]
    seq_len = total_rows // NSEQ
    n_x = lax.axis_size("x")
    partial_logits = lax.dot_general(
        gathered,
        head_weight,
        (((1,), (1,)), ((), ())),
        preferred_element_type=jnp.float32,
    )
    logits = _reduce_scatter_a2a(partial_logits, SEC)
    logits = with_layout_constraint(logits, Layout((0, 1)))
    columns = logits.shape[1]
    soft = jax.nn.softplus(logits)
    act = jnp.log1p(soft)
    positions = jnp.arange(seq_len, dtype=jnp.int32)
    live = (positions[None, :] < lengths[:, None]).astype(jnp.float32)
    expo = jnp.exp(act / pool_temp).reshape(NSEQ, seq_len, columns) * live[:, :, None]
    totals = jnp.sum(expo, axis=1)
    pooled = pool_temp * jnp.log(totals)
    queries = pooled[:half]
    documents = pooled[half:]
    dots_part = lax.dot_general(
        queries, documents, (((1,), (1,)), ((), ())), precision=lax.Precision.HIGHEST
    )
    norms_part = jnp.sum(pooled * pooled, axis=1)
    stats = jnp.concatenate([dots_part.reshape(-1), norms_part])
    for axes in (VOC, SEC):
        stats = _all_reduce_a2a(stats, axes)
    dots = stats[: half * half].reshape(half, half)
    norms = stats[half * half :]
    inv = lax.rsqrt(norms + eps_norm)
    inv_q = inv[:half]
    inv_d = inv[half:]
    scores = dots * inv_q[:, None] * inv_d[None, :] / score_temp
    weights = jnp.exp(scores)
    row_sum = jnp.sum(weights, axis=1)
    probs = weights / row_sum[:, None]
    target = (jnp.arange(half, dtype=jnp.int32)[None, :] == pairing[:, None]).astype(jnp.float32)
    loss = jnp.sum(jnp.log(row_sum) - jnp.sum(scores * target, axis=1))
    dscore = grad_scale * (probs - target)
    gdots = dscore * inv_q[:, None] * inv_d[None, :] / score_temp
    dinv_q = jnp.sum(dscore * dots * inv_d[None, :], axis=1) / score_temp
    dinv_d = jnp.sum(dscore * dots * inv_q[:, None], axis=0) / score_temp
    dinv = jnp.concatenate([dinv_q, dinv_d])
    dnorm = -0.5 * dinv * inv * inv * inv
    dpool_q = (
        jnp.dot(gdots, documents, precision=lax.Precision.HIGHEST)
        + 2.0 * dnorm[:half, None] * queries
    )
    dpool_d = (
        jnp.dot(gdots.T, queries, precision=lax.Precision.HIGHEST)
        + 2.0 * dnorm[half:, None] * documents
    )
    dpooled = jnp.concatenate([dpool_q, dpool_d], axis=0)
    dact = (dpooled[:, None, :] * expo / totals[:, None, :]).reshape(total_rows, columns)
    dlogit = (dact * jax.nn.sigmoid(logits) / (1.0 + soft)).astype(jnp.bfloat16)
    dlogit = with_layout_constraint(dlogit, Layout((0, 1)))
    n_sec = _members(SEC)
    copies = jnp.broadcast_to(dlogit.T[None], (n_sec,) + dlogit.T.shape)
    copies = with_layout_constraint(copies, Layout((0, 1, 2)))
    dlogit_t = lax.all_to_all(copies, SEC, 0, 0, tiled=True).reshape(-1, dlogit.shape[0])
    grad_t = lax.dot_general(
        head_weight, dlogit_t, (((0,), (0,)), ((), ())), preferred_element_type=jnp.float32
    )
    n_zl, n_yl, n_c = (lax.axis_size(a) for a in near)
    rows = hidden.shape[0]
    width = grad_t.shape[0]
    grad = grad_t.reshape(width, n_zh, n_zl, n_yl, n_c, rows).transpose(4, 1, 2, 3, 0, 5)
    grad = jnp.sum(lax.all_to_all(grad, "c", 0, 0, tiled=True), axis=0)
    grad = grad.transpose(1, 2, 0, 3, 4).reshape(n_zl * n_yl, n_zh, width, rows)
    grad = jnp.sum(lax.all_to_all(grad, ("zl", "yl"), 0, 0, tiled=True), axis=0)
    me = lax.axis_index("zh")
    hidden_grad = lax.dynamic_index_in_dim(grad, me, 0, keepdims=False)
    for k in range(1, n_zh):
        block = lax.dynamic_index_in_dim(grad, (me + k) % n_zh, 0, keepdims=False)
        hidden_grad = hidden_grad + _shift(block, "zh", n_zh, k)
    hidden_grad = hidden_grad.T
    return (hidden_grad, loss)


def solution(mesh):
    n_sec, n_voc = mesh.devices.shape
    fine = Mesh(
        mesh.devices.reshape(n_sec // 2, 2, n_voc // 16, 4, 2, 2), SEC + VOC
    )
    in_specs = (P(VOC, SEC), P(VOC, SEC), P(), P())
    out_specs = (P(VOC, SEC), P())
    return jax.shard_map(local, mesh=fine, in_specs=in_specs, out_specs=out_specs, check_vma=False)
```
